512 devices in a mesh: ctx: 16 (over y, x_hi), tp: 32 (over z, x_lo, core).
Axes of the slice: x: 4 (x_hi: 2, x_lo: 2; x = x_hi * 2 + x_lo), y: 8, z: 8, core: 2. Of those that a mesh axis runs over, the one named last changes fastest.
Arguments:
- resid_in: bfloat16 [2048, 4096], P('ctx', 'tp'), may hold values from -6 to 6
- feats: bfloat16 [2048, 3, 4096], P('ctx', None, 'tp'), may hold values from -6 to 6
- short_filter: float32 [3, 3, 4096], P(None, None, 'tp'), may hold values from -3.5 to 3.5
- residues: float32 [4096, 16], P('tp'), may hold values from -4 to 4
- rates: float32 [4096, 16], P('tp'), may hold values from 0.00014648438 to 0.03
- out_weight: bfloat16 [4096, 4096], P('tp'), may hold values from -0.1875 to 0.1875
- norm_gain: float32 [4096], replicated, may hold values from 0.1 to 1.9
- attn_weight: bfloat16 [4096, 3, 4096], P(None, None, 'tp'), may hold values from -1 to 1
Outputs:
- hyena_out: bfloat16 [2048, 4096], P('ctx', 'tp')
- context: bfloat16 [2048, 4096], P('ctx', 'tp')
The draws below stay inside these ranges and needn't reach their ends.
All inputs are finite; a program needn't handle non-finite values.
Results may differ from the reference program's by a relative error of at most 0.01.
Values may be sent and summed in bfloat16 or wider, within the bound.
No kernel may reach another device: no remote copies, remote signals or barrier semaphores. Data moves between devices by JAX's collectives and lax.ppermute only.
A program may use at most 192 MiB of HBM per device.

```python
import math
import jax
import jax.numpy as jnp
from jax import lax

HEAD_DIM = 128
MODES = 16
D = 4096
SEQ = 2048


def draw_attn_weight(key, part):
    first_key = jax.random.fold_in(jax.random.fold_in(key, 7), 0)
    joined = jax.random.normal(first_key, (D, 3, D), jnp.float32) / math.sqrt(D)
    return jnp.clip(joined, -1.0, 1.0).astype(jnp.bfloat16)


def raised(values, rng, source, target, blocks, factor):
    def block_of(dim):
        return (jnp.arange(values.shape[dim]) // (values.shape[dim] // blocks)).reshape((-1,) + (1,) * (values.ndim - 1 - dim))

    one_side = jax.random.permutation(rng, blocks)[block_of(target)]
    other_side = (block_of(target) + blocks // 2) % blocks
    return jnp.where((block_of(source) == one_side) | (block_of(source) == other_side), factor * values, values)


def block_levels(stream_key, dims, cuts, smallest, high):
    level = 1.0
    for position, blocks in cuts:
        heights = jax.random.uniform(jax.random.fold_in(jax.random.fold_in(stream_key, 6), position), (blocks,), jnp.float32, smallest / len(cuts), high / len(cuts))
        level = level * jnp.repeat(jnp.exp(heights), dims[position] // blocks).reshape((-1,) + (1,) * (len(dims) - 1 - position))
    return level


def scatter_about(rng, dims, scale, reach, shards=(), held_as=jnp.bfloat16):
    array = jax.random.normal(rng, dims, jnp.float32) * scale
    if len(shards) > 0:
        array = block_levels(rng, dims, shards, -0.22, 0.18) * array
    return jnp.clip(array, min=-reach, max=reach).astype(held_as)


def noise_with(own_key, dims, scale, bound, shards, heavy, held_as=jnp.bfloat16):
    result = scale * jax.random.normal(own_key, dims, jnp.float32)
    if shards:
        result = result * block_levels(own_key, dims, shards, -0.22, 0.18)
    return jnp.clip(raised(result, jax.random.fold_in(own_key, 3), *heavy), -bound, bound).astype(held_as)


def setup_inputs(seed: int = 0) -> dict:
    splits = jax.random.split(jax.random.key(seed), 9)
    resid_in = scatter_about(splits[0], (SEQ, D), 1.0, 6.0, ((0, 16), (1, 32)))
    feats = scatter_about(splits[1], (SEQ, 3, D), 1.0, 6.0, ((0, 16), (2, 32)))
    short_filter = scatter_about(splits[2], (3, 3, D), 3 ** -0.5, 3.5, ((2, 32),), jnp.float32)
    residues = scatter_about(splits[3], (D, MODES), 0.25, 4.0, ((0, 32),), jnp.float32)
    rates = jnp.clip(jnp.exp(math.log(0.03) - 5.322034 * jax.random.uniform(splits[4], (D, MODES), jnp.float32) ** block_levels(splits[4], (D, MODES), ((0, 32),), -0.2, 0.2)), 0.00014648438, 0.03)
    out_weight = noise_with(splits[5], (D, D), D ** -0.5, 0.1875, ((0, 32),), (0, 1, 32, 2.75))
    norm_gain = jnp.clip(1.0 + 0.18 * jax.random.normal(splits[6], (D,), jnp.float32), 0.1, 1.9)
    attn_weight = draw_attn_weight(jax.random.fold_in(splits[8], 71), 0)
    return {"resid_in": resid_in, "feats": feats, "short_filter": short_filter, "residues": residues, "rates": rates, "out_weight": out_weight, "norm_gain": norm_gain, "attn_weight": attn_weight}


def long_conv(signal, residues, rates):
    seq_total, width_all = signal.shape
    block_size = math.gcd(width_all, 256)
    block_count = width_all // block_size
    lag_steps = jnp.arange(seq_total, dtype=jnp.float32)
    fft_size = 2 * seq_total

    def one_block(slot_item):
        sig_block, res_block, rate_block = slot_item
        weight = res_block * jnp.sqrt(1.0 - jnp.exp(-2.0 * rate_block))
        filter_taps = lax.optimization_barrier(jnp.sum(weight[:, :, None] * jnp.exp(-rate_block[:, :, None] * lag_steps), axis=1))
        spectrum = jnp.fft.rfft(sig_block.T.astype(jnp.float32), n=fft_size) * jnp.fft.rfft(filter_taps, n=fft_size)
        return jnp.fft.irfft(spectrum, n=fft_size)[:, :seq_total]
    sig_parts = signal.reshape(seq_total, block_count, block_size).transpose(1, 0, 2)
    res_parts = residues.reshape(block_count, block_size, residues.shape[1])
    rate_parts = rates.reshape(block_count, block_size, rates.shape[1])
    outputs = lax.map(one_block, (sig_parts, res_parts, rate_parts))
    return outputs.transpose(2, 0, 1).reshape(seq_total, width_all)

def rotary_turn(vectors, positions):
    half_dim = vectors.shape[-1] // 2
    frequency = 10000.0 ** (-jnp.arange(half_dim, dtype=jnp.float32) * 2.0 / vectors.shape[-1])
    angles = positions.astype(jnp.float32)[:, None] * frequency[None, :]
    cosine = jnp.cos(angles)[:, None, :]
    sine_part = jnp.sin(angles)[:, None, :]
    first_half = vectors[..., :half_dim]
    second = vectors[..., half_dim:]
    return jnp.concatenate([first_half * cosine - second * sine_part, second * cosine + first_half * sine_part], axis=-1)

def reference(resid_in, feats, short_filter, residues, rates, out_weight, norm_gain, attn_weight):
    seq_total = feats.shape[0]
    width_all = feats.shape[2]
    as_float = feats.astype(jnp.float32)
    padded = jnp.concatenate([jnp.zeros((2, 3, width_all), jnp.float32), as_float], axis=0)
    short_out = short_filter[0] * padded[2:] + short_filter[1] * padded[1:seq_total + 1] + short_filter[2] * padded[:seq_total]
    product = (short_out[:, 1] * short_out[:, 2]).astype(jnp.bfloat16)
    conv_out = long_conv(product, residues, rates)
    gated = (short_out[:, 0] * conv_out).astype(jnp.bfloat16)
    mix = jnp.dot(gated, out_weight, preferred_element_type=jnp.float32)
    hyena_out = (resid_in.astype(jnp.float32) + mix).astype(jnp.bfloat16)
    wide = hyena_out.astype(jnp.float32)
    mean_square = lax.optimization_barrier(jnp.mean(wide * wide, axis=1, keepdims=True))
    normed = (wide * lax.rsqrt(mean_square + 1e-05) * norm_gain).astype(jnp.bfloat16)
    projected = jnp.dot(normed, attn_weight.reshape(width_all, 3 * width_all), preferred_element_type=jnp.float32).reshape(seq_total, 3, width_all)
    head_count = width_all // HEAD_DIM
    positions = jnp.arange(seq_total, dtype=jnp.int32)
    queries = rotary_turn(projected[:, 0].reshape(seq_total, head_count, HEAD_DIM), positions).astype(jnp.bfloat16)
    keys_all = rotary_turn(projected[:, 1].reshape(seq_total, head_count, HEAD_DIM), positions).astype(jnp.bfloat16)
    values = projected[:, 2].reshape(seq_total, head_count, HEAD_DIM).astype(jnp.bfloat16)
    score_scale = 1.0 / math.sqrt(HEAD_DIM)
    block_size = math.gcd(seq_total, 1024)
    block_count = seq_total // block_size
    key_pos = jnp.arange(seq_total, dtype=jnp.int32)

    def one_head(slot_item):
        head_queries, head_keys, head_values = slot_item
        query_blocks = head_queries.reshape(block_count, block_size, HEAD_DIM)

        def one_block(pair_item):
            query_block, block_index = pair_item
            scores = jnp.dot(query_block, head_keys.T, preferred_element_type=jnp.float32) * score_scale
            query_pos = block_index * block_size + jnp.arange(block_size, dtype=jnp.int32)
            allowed = query_pos[:, None] >= key_pos[None, :]
            masked = jnp.where(allowed, scores, -1e+30)
            run_peak = lax.optimization_barrier(jnp.max(masked, axis=1, keepdims=True))
            probs = jnp.where(allowed, jnp.exp(masked - run_peak), 0.0)
            denom = lax.optimization_barrier(jnp.sum(probs, axis=1, keepdims=True))
            summed = jnp.dot(probs.astype(jnp.bfloat16), head_values, preferred_element_type=jnp.float32)
            return summed / denom
        outputs = lax.map(one_block, (query_blocks, jnp.arange(block_count, dtype=jnp.int32)))
        return outputs.reshape(seq_total, HEAD_DIM)
    per_head = lax.map(one_head, (queries.transpose(1, 0, 2), keys_all.transpose(1, 0, 2), values.transpose(1, 0, 2)))
    context = per_head.transpose(1, 0, 2).reshape(seq_total, width_all).astype(jnp.bfloat16)
    return (hyena_out, context)
```

```python
import math

import jax
import jax.numpy as jnp
from jax import lax
from jax.sharding import PartitionSpec as P

HEAD_DIM = 128


eps_norm = 1e-05
rope_base = 10000.0
mask_fill = -1e30
highest = lax.Precision.HIGHEST


def shifted(value, axis, steps):
    count = lax.axis_size(axis)
    initial, last = (max(0, -steps), min(count, count - steps))
    return lax.ppermute(value, axis, [(source, source + steps) for source in range(initial, last)])


def gather_by_exchange(block, axis, concat_axis=1):
    count = lax.axis_size(axis)
    copies = jnp.broadcast_to(block[None], (count,) + block.shape)
    return lax.all_to_all(copies, axis, split_axis=0, concat_axis=concat_axis, tiled=False)


def toeplitz_lower(filter_taps):
    chan_count, block_size = filter_taps.shape
    padded = jnp.concatenate(
        [jnp.zeros((chan_count, block_size - 1), jnp.float32), filter_taps], axis=1
    )
    flipped = padded[:, ::-1]
    tiled = jnp.tile(flipped, (1, block_size))
    offset = block_size - 1
    window = tiled[:, offset : offset + block_size * (2 * block_size - 2)]
    return window.reshape(chan_count, block_size, 2 * block_size - 2)[:, :, :block_size]


def modal_conv(signal, residues, rates, start_state):
    chan_count, length = signal.shape
    block_size = math.gcd(length, 128)
    block_count = length // block_size
    weight = residues * jnp.sqrt(1.0 - jnp.exp(-2.0 * rates))
    lag_steps = jnp.arange(block_size, dtype=jnp.float32)
    powers = jnp.exp(-rates[:, :, None] * lag_steps)
    filter_taps = jnp.sum(weight[:, :, None] * powers, axis=1)
    toeplitz = toeplitz_lower(filter_taps)
    blocks = signal.reshape(chan_count, block_count, block_size)
    inner_part = jnp.einsum("cij,cnj->cni", toeplitz, blocks, precision=highest)
    tail_powers = jnp.exp(-rates[:, :, None] * (block_size - lag_steps))
    end_states = jnp.einsum("cnj,cmj->cnm", blocks, tail_powers, precision=highest)
    block_steps = jnp.arange(block_count, dtype=jnp.float32)
    gap_count = block_steps[:, None] - 1.0 - block_steps[None, :]
    live_mask = gap_count >= 0.0
    carry_mat = jnp.where(
        live_mask, jnp.exp(-rates[:, :, None, None] * block_size * jnp.maximum(gap_count, 0.0)), 0.0
    )
    states = jnp.einsum("cmnk,ckm->cnm", carry_mat, end_states, precision=highest)
    states = (
        states
        + jnp.exp(-rates[:, None, :] * block_size * block_steps[None, :, None])
        * start_state[:, None, :]
    )
    cross_part = jnp.einsum("cnm,cmi->cni", states * weight[:, None, :], powers, precision=highest)
    return (inner_part + cross_part).reshape(chan_count, length)


def short_mix(feats, short_filter):
    row_count = feats.shape[0]
    prior_feats = shifted(feats[-2:], "ctx", 1)
    joined = jnp.concatenate([prior_feats, feats], axis=0).astype(jnp.float32)
    return (
        short_filter[0] * joined[2:]
        + short_filter[1] * joined[1 : row_count + 1]
        + short_filter[2] * joined[:row_count]
    )


def rotary_turn(vectors, positions):
    half_dim = vectors.shape[-1] // 2
    frequency = rope_base ** (-jnp.arange(half_dim, dtype=jnp.float32) * 2.0 / vectors.shape[-1])
    angles = positions.astype(jnp.float32)[:, None] * frequency[None, :]
    cosine = jnp.cos(angles)[:, None, :]
    sine_part = jnp.sin(angles)[:, None, :]
    first_half = vectors[..., :half_dim]
    second = vectors[..., half_dim:]
    return jnp.concatenate(
        [first_half * cosine - second * sine_part, second * cosine + first_half * sine_part],
        axis=-1,
    )


def attend_tile(running, query_rows, query_pos, key_block, value_block, key_start):
    run_peak, denom, accumulated = running
    block_size = key_block.shape[0]
    score_scale = 1.0 / math.sqrt(key_block.shape[2])
    key_pos = key_start + jnp.arange(block_size, dtype=jnp.int32)
    scores = (
        jnp.einsum("shd,khd->hsk", query_rows, key_block, preferred_element_type=jnp.float32)
        * score_scale
    )
    allowed = (query_pos[:, None] >= key_pos[None, :])[None]
    masked = jnp.where(allowed, scores, mask_fill)
    new_peak = jnp.maximum(run_peak, jnp.max(masked, axis=2))
    weights = jnp.where(allowed, jnp.exp(masked - new_peak[:, :, None]), 0.0)
    factor = jnp.exp(run_peak - new_peak)
    denom = denom * factor + jnp.sum(weights, axis=2)
    accumulated = accumulated * factor[:, :, None] + jnp.einsum(
        "hsk,khd->hsd",
        weights.astype(jnp.bfloat16),
        value_block,
        preferred_element_type=jnp.float32,
    )
    return (new_peak, denom, accumulated)


def empty_state(head_count, rows):
    return (
        jnp.full((head_count, rows), mask_fill, jnp.float32),
        jnp.zeros((head_count, rows), jnp.float32),
        jnp.zeros((head_count, rows, HEAD_DIM), jnp.float32),
    )


def finish_rows(state):
    run_peak, denom, accumulated = state
    heads_out = accumulated / denom[:, :, None]
    rows = heads_out.shape[1]
    return (
        heads_out.transpose(1, 0, 2)
        .reshape(rows, heads_out.shape[0] * heads_out.shape[2])
        .astype(jnp.bfloat16)
    )


def per_device(resid_in, feats, short_filter, residues, rates, out_weight, norm_gain, attn_weight):
    row_count, chan_count = resid_in.shape
    width_all = out_weight.shape[1]
    short_out = short_mix(feats, short_filter)
    product = (short_out[:, 1] * short_out[:, 2]).astype(jnp.bfloat16)
    panel_rows = lax.all_to_all(product.T, "ctx", split_axis=0, concat_axis=1, tiled=True)
    panel_count = chan_count // lax.axis_size("ctx")
    panel_start = lax.axis_index("ctx") * panel_count
    panel_res = lax.dynamic_slice_in_dim(residues, panel_start, panel_count, 0)
    panel_rates = lax.dynamic_slice_in_dim(rates, panel_start, panel_count, 0)
    panel_conv = modal_conv(
        panel_rows.astype(jnp.float32), panel_res, panel_rates, jnp.zeros_like(panel_rates)
    )
    returned = lax.all_to_all(panel_conv, "ctx", split_axis=1, concat_axis=0, tiled=True)
    conv_out = returned.T
    gated = (short_out[:, 0] * conv_out).astype(jnp.bfloat16)
    tp_count = lax.axis_size("tp")
    partials = lax.dot_general(
        out_weight, gated, (((0,), (1,)), ((), ())), preferred_element_type=jnp.float32
    ).astype(jnp.bfloat16)
    received = lax.all_to_all(partials, "tp", split_axis=0, concat_axis=0, tiled=True)
    own_share = jnp.sum(
        received.reshape(tp_count, chan_count, row_count).astype(jnp.float32), axis=0
    )
    hyena_out = (resid_in.astype(jnp.float32) + own_share.T).astype(jnp.bfloat16)
    full_rows = gather_by_exchange(hyena_out, "tp").reshape(row_count, width_all)
    wide = full_rows.astype(jnp.float32)
    mean_square = jnp.mean(wide * wide, axis=1, keepdims=True)
    normed = (wide * lax.rsqrt(mean_square + eps_norm) * norm_gain).astype(jnp.bfloat16)
    projected = jnp.dot(
        normed, attn_weight.reshape(width_all, 3 * chan_count), preferred_element_type=jnp.float32
    ).reshape(row_count, 3, chan_count)
    head_count = chan_count // HEAD_DIM
    ctx_index = lax.axis_index("ctx")
    first_pos = ctx_index * row_count
    positions = first_pos + jnp.arange(row_count, dtype=jnp.int32)
    queries = rotary_turn(
        projected[:, 0].reshape(row_count, head_count, HEAD_DIM), positions
    ).astype(jnp.bfloat16)
    keys_all = rotary_turn(
        projected[:, 1].reshape(row_count, head_count, HEAD_DIM), positions
    ).astype(jnp.bfloat16)
    values = projected[:, 2].astype(jnp.bfloat16)
    key_pieces = (keys_all.reshape(row_count, chan_count), values)
    initial = empty_state(head_count, row_count)
    joined_kv = jnp.concatenate(key_pieces, axis=1)
    gathered_kv = gather_by_exchange(joined_kv, "ctx", concat_axis=0)
    gathered_kv = gathered_kv.reshape(lax.axis_size("ctx") * row_count, 2 * chan_count)
    key_rows = gathered_kv[:, :chan_count]
    value_rows = gathered_kv[:, chan_count:]
    key_total = key_rows.shape[0]
    tiles_block_size = math.gcd(key_total, 1024)
    block_count = key_total // tiles_block_size
    key_blocks = key_rows.reshape(block_count, tiles_block_size, head_count, HEAD_DIM)
    value_blocks = value_rows.reshape(block_count, tiles_block_size, head_count, HEAD_DIM)
    key_blocks, value_blocks, block_ids, block_size = (
        key_blocks,
        value_blocks,
        jnp.arange(block_count, dtype=jnp.int32),
        tiles_block_size,
    )

    def one_tile(carried, slot_item):
        key_block, value_block, block_index = slot_item
        key_start = block_index * block_size
        updated = attend_tile(carried, queries, positions, key_block, value_block, key_start)
        return (updated, None)

    result, _ = lax.scan(one_tile, initial, (key_blocks, value_blocks, block_ids))
    context = finish_rows(result)
    return (hyena_out, context)


def solution(mesh):
    in_specs = (
        P("ctx", "tp"),
        P("ctx", None, "tp"),
        P(None, None, "tp"),
        P("tp", None),
        P("tp", None),
        P("tp", None),
        P(),
        P(None, None, "tp"),
    )
    out_specs = (P("ctx", "tp"), P("ctx", "tp"))
    return jax.shard_map(
        per_device, mesh=mesh, in_specs=in_specs, out_specs=out_specs, check_vma=False
    )
```

```python
import math

import jax
import jax.numpy as jnp
from jax import lax
from jax.sharding import PartitionSpec as P

HEAD_DIM = 128


eps_norm = 1e-05
rope_base = 10000.0
mask_fill = -1e30
highest = lax.Precision.HIGHEST


def shifted(value, axis, steps):
    count = lax.axis_size(axis)
    initial, last = (max(0, -steps), min(count, count - steps))
    return lax.ppermute(value, axis, [(source, source + steps) for source in range(initial, last)])


def gather_by_exchange(block, axis, concat_axis=1):
    count = lax.axis_size(axis)
    copies = jnp.broadcast_to(block[None], (count,) + block.shape)
    return lax.all_to_all(copies, axis, split_axis=0, concat_axis=concat_axis, tiled=False)


def toeplitz_lower(filter_taps):
    chan_count, block_size = filter_taps.shape
    padded = jnp.concatenate(
        [jnp.zeros((chan_count, block_size - 1), jnp.float32), filter_taps], axis=1
    )
    flipped = padded[:, ::-1]
    tiled = jnp.tile(flipped, (1, block_size))
    offset = block_size - 1
    window = tiled[:, offset : offset + block_size * (2 * block_size - 2)]
    return window.reshape(chan_count, block_size, 2 * block_size - 2)[:, :, :block_size]


def modal_conv(signal, residues, rates, start_state):
    chan_count, length = signal.shape
    block_size = math.gcd(length, 128)
    block_count = length // block_size
    weight = residues * jnp.sqrt(1.0 - jnp.exp(-2.0 * rates))
    lag_steps = jnp.arange(block_size, dtype=jnp.float32)
    powers = jnp.exp(-rates[:, :, None] * lag_steps)
    filter_taps = jnp.sum(weight[:, :, None] * powers, axis=1)
    toeplitz = toeplitz_lower(filter_taps)
    blocks = signal.reshape(chan_count, block_count, block_size)
    inner_part = jnp.einsum("cij,cnj->cni", toeplitz, blocks, precision=highest)
    tail_powers = jnp.exp(-rates[:, :, None] * (block_size - lag_steps))
    end_states = jnp.einsum("cnj,cmj->cnm", blocks, tail_powers, precision=highest)
    block_steps = jnp.arange(block_count, dtype=jnp.float32)
    gap_count = block_steps[:, None] - 1.0 - block_steps[None, :]
    live_mask = gap_count >= 0.0
    carry_mat = jnp.where(
        live_mask, jnp.exp(-rates[:, :, None, None] * block_size * jnp.maximum(gap_count, 0.0)), 0.0
    )
    states = jnp.einsum("cmnk,ckm->cnm", carry_mat, end_states, precision=highest)
    states = (
        states
        + jnp.exp(-rates[:, None, :] * block_size * block_steps[None, :, None])
        * start_state[:, None, :]
    )
    cross_part = jnp.einsum("cnm,cmi->cni", states * weight[:, None, :], powers, precision=highest)
    return (inner_part + cross_part).reshape(chan_count, length)


def short_mix(feats, short_filter):
    row_count = feats.shape[0]
    prior_feats = shifted(feats[-2:], "ctx", 1)
    joined = jnp.concatenate([prior_feats, feats], axis=0).astype(jnp.float32)
    return (
        short_filter[0] * joined[2:]
        + short_filter[1] * joined[1 : row_count + 1]
        + short_filter[2] * joined[:row_count]
    )


def rotary_turn(vectors, positions):
    half_dim = vectors.shape[-1] // 2
    frequency = rope_base ** (-jnp.arange(half_dim, dtype=jnp.float32) * 2.0 / vectors.shape[-1])
    angles = positions.astype(jnp.float32)[:, None] * frequency[None, :]
    cosine = jnp.cos(angles)[:, None, :]
    sine_part = jnp.sin(angles)[:, None, :]
    first_half = vectors[..., :half_dim]
    second = vectors[..., half_dim:]
    return jnp.concatenate(
        [first_half * cosine - second * sine_part, second * cosine + first_half * sine_part],
        axis=-1,
    )


def attend_tile(running, query_rows, query_pos, key_block, value_block, key_start):
    run_peak, denom, accumulated = running
    block_size = key_block.shape[0]
    score_scale = 1.0 / math.sqrt(key_block.shape[2])
    key_pos = key_start + jnp.arange(block_size, dtype=jnp.int32)
    scores = (
        jnp.einsum("shd,khd->hsk", query_rows, key_block, preferred_element_type=jnp.float32)
        * score_scale
    )
    allowed = (query_pos[:, None] >= key_pos[None, :])[None]
    masked = jnp.where(allowed, scores, mask_fill)
    new_peak = jnp.maximum(run_peak, jnp.max(masked, axis=2))
    weights = jnp.where(allowed, jnp.exp(masked - new_peak[:, :, None]), 0.0)
    factor = jnp.exp(run_peak - new_peak)
    denom = denom * factor + jnp.sum(weights, axis=2)
    accumulated = accumulated * factor[:, :, None] + jnp.einsum(
        "hsk,khd->hsd",
        weights.astype(jnp.bfloat16),
        value_block,
        preferred_element_type=jnp.float32,
    )
    return (new_peak, denom, accumulated)


def empty_state(head_count, rows):
    return (
        jnp.full((head_count, rows), mask_fill, jnp.float32),
        jnp.zeros((head_count, rows), jnp.float32),
        jnp.zeros((head_count, rows, HEAD_DIM), jnp.float32),
    )


def finish_rows(state):
    run_peak, denom, accumulated = state
    heads_out = accumulated / denom[:, :, None]
    rows = heads_out.shape[1]
    return (
        heads_out.transpose(1, 0, 2)
        .reshape(rows, heads_out.shape[0] * heads_out.shape[2])
        .astype(jnp.bfloat16)
    )


def per_device(resid_in, feats, short_filter, residues, rates, out_weight, norm_gain, attn_weight):
    row_count, chan_count = resid_in.shape
    width_all = out_weight.shape[1]
    short_out = short_mix(feats, short_filter)
    product = (short_out[:, 1] * short_out[:, 2]).astype(jnp.bfloat16)
    signal = product.T.astype(jnp.float32)
    lag_steps = jnp.arange(row_count, dtype=jnp.float32)
    tail_powers = jnp.exp(-rates[:, :, None] * (row_count - lag_steps))
    end_state = jnp.einsum("ct,cmt->cm", signal, tail_powers, precision=highest)
    gathered_states = gather_by_exchange(end_state, "ctx", concat_axis=0)
    shard_steps = jnp.arange(lax.axis_size("ctx"), dtype=jnp.float32)
    gap_count = lax.axis_index("ctx").astype(jnp.float32) - 1.0 - shard_steps
    decay = jnp.where(
        (gap_count >= 0.0)[:, None, None],
        jnp.exp(-rates[None] * row_count * jnp.maximum(gap_count, 0.0)[:, None, None]),
        0.0,
    )
    start_state = jnp.sum(decay * gathered_states, axis=0)
    conv_out = modal_conv(signal, residues, rates, start_state).T
    gated = (short_out[:, 0] * conv_out).astype(jnp.bfloat16)
    tp_count = lax.axis_size("tp")
    partials = lax.dot_general(
        out_weight, gated, (((0,), (1,)), ((), ())), preferred_element_type=jnp.float32
    ).astype(jnp.bfloat16)
    received = lax.all_to_all(partials, "tp", split_axis=0, concat_axis=0, tiled=True)
    own_share = jnp.sum(
        received.reshape(tp_count, chan_count, row_count).astype(jnp.float32), axis=0
    )
    hyena_out = (resid_in.astype(jnp.float32) + own_share.T).astype(jnp.bfloat16)
    full_rows = gather_by_exchange(hyena_out, "tp").reshape(row_count, width_all)
    wide = full_rows.astype(jnp.float32)
    mean_square = jnp.mean(wide * wide, axis=1, keepdims=True)
    normed = (wide * lax.rsqrt(mean_square + eps_norm) * norm_gain).astype(jnp.bfloat16)
    projected = jnp.dot(
        normed, attn_weight.reshape(width_all, 3 * chan_count), preferred_element_type=jnp.float32
    ).reshape(row_count, 3, chan_count)
    head_count = chan_count // HEAD_DIM
    ctx_index = lax.axis_index("ctx")
    first_pos = ctx_index * row_count
    positions = first_pos + jnp.arange(row_count, dtype=jnp.int32)
    queries = rotary_turn(
        projected[:, 0].reshape(row_count, head_count, HEAD_DIM), positions
    ).astype(jnp.bfloat16)
    keys_all = rotary_turn(
        projected[:, 1].reshape(row_count, head_count, HEAD_DIM), positions
    ).astype(jnp.bfloat16)
    values = projected[:, 2].astype(jnp.bfloat16)
    key_pieces = (keys_all.reshape(row_count, chan_count), values)
    initial = empty_state(head_count, row_count)
    joined_kv = jnp.concatenate(key_pieces, axis=1)
    gathered_kv = gather_by_exchange(joined_kv, "ctx", concat_axis=0)
    gathered_kv = gathered_kv.reshape(lax.axis_size("ctx") * row_count, 2 * chan_count)
    key_rows = gathered_kv[:, :chan_count]
    value_rows = gathered_kv[:, chan_count:]
    key_total = key_rows.shape[0]
    tiles_block_size = math.gcd(key_total, 1024)
    block_count = key_total // tiles_block_size
    key_blocks = key_rows.reshape(block_count, tiles_block_size, head_count, HEAD_DIM)
    value_blocks = value_rows.reshape(block_count, tiles_block_size, head_count, HEAD_DIM)
    key_blocks, value_blocks, block_ids, block_size = (
        key_blocks,
        value_blocks,
        jnp.arange(block_count, dtype=jnp.int32),
        tiles_block_size,
    )

    def one_tile(carried, slot_item):
        key_block, value_block, block_index = slot_item
        key_start = block_index * block_size
        updated = attend_tile(carried, queries, positions, key_block, value_block, key_start)
        return (updated, None)

    result, _ = lax.scan(one_tile, initial, (key_blocks, value_blocks, block_ids))
    context = finish_rows(result)
    return (hyena_out, context)


def solution(mesh):
    in_specs = (
        P("ctx", "tp"),
        P("ctx", None, "tp"),
        P(None, None, "tp"),
        P("tp", None),
        P("tp", None),
        P("tp", None),
        P(),
        P(None, None, "tp"),
    )
    out_specs = (P("ctx", "tp"), P("ctx", "tp"))
    return jax.shard_map(
        per_device, mesh=mesh, in_specs=in_specs, out_specs=out_specs, check_vma=False
    )
```

```python
import math

import jax
import jax.numpy as jnp
from jax import lax
from jax.sharding import PartitionSpec as P

HEAD_DIM = 128


eps_norm = 1e-05
rope_base = 10000.0
mask_fill = -1e30
highest = lax.Precision.HIGHEST


def shifted(value, axis, steps):
    count = lax.axis_size(axis)
    initial, last = (max(0, -steps), min(count, count - steps))
    return lax.ppermute(value, axis, [(source, source + steps) for source in range(initial, last)])


def gather_by_exchange(block, axis, concat_axis=1):
    count = lax.axis_size(axis)
    copies = jnp.broadcast_to(block[None], (count,) + block.shape)
    return lax.all_to_all(copies, axis, split_axis=0, concat_axis=concat_axis, tiled=False)


def toeplitz_lower(filter_taps):
    chan_count, block_size = filter_taps.shape
    padded = jnp.concatenate(
        [jnp.zeros((chan_count, block_size - 1), jnp.float32), filter_taps], axis=1
    )
    flipped = padded[:, ::-1]
    tiled = jnp.tile(flipped, (1, block_size))
    offset = block_size - 1
    window = tiled[:, offset : offset + block_size * (2 * block_size - 2)]
    return window.reshape(chan_count, block_size, 2 * block_size - 2)[:, :, :block_size]


def modal_conv(signal, residues, rates, start_state, block_limit=128):
    chan_count, length = signal.shape
    block_size = math.gcd(length, block_limit)
    block_count = length // block_size
    weight = residues * jnp.sqrt(1.0 - jnp.exp(-2.0 * rates))
    lag_steps = jnp.arange(block_size, dtype=jnp.float32)
    powers = jnp.exp(-rates[:, :, None] * lag_steps)
    filter_taps = jnp.sum(weight[:, :, None] * powers, axis=1)
    toeplitz = toeplitz_lower(filter_taps)
    blocks = signal.reshape(chan_count, block_count, block_size)
    inner_part = jnp.einsum("cij,cnj->cni", toeplitz, blocks, precision=highest)
    tail_powers = jnp.exp(-rates[:, :, None] * (block_size - lag_steps))
    end_states = jnp.einsum("cnj,cmj->cnm", blocks, tail_powers, precision=highest)
    block_steps = jnp.arange(block_count, dtype=jnp.float32)
    gap_count = block_steps[:, None] - 1.0 - block_steps[None, :]
    live_mask = gap_count >= 0.0
    carry_mat = jnp.where(
        live_mask, jnp.exp(-rates[:, :, None, None] * block_size * jnp.maximum(gap_count, 0.0)), 0.0
    )
    states = jnp.einsum("cmnk,ckm->cnm", carry_mat, end_states, precision=highest)
    states = (
        states
        + jnp.exp(-rates[:, None, :] * block_size * block_steps[None, :, None])
        * start_state[:, None, :]
    )
    cross_part = jnp.einsum("cnm,cmi->cni", states * weight[:, None, :], powers, precision=highest)
    return (inner_part + cross_part).reshape(chan_count, length)


def short_mix(feats, short_filter):
    row_count = feats.shape[0]
    prior_feats = shifted(feats[-2:], "ctx", 1)
    joined = jnp.concatenate([prior_feats, feats], axis=0).astype(jnp.float32)
    return (
        short_filter[0] * joined[2:]
        + short_filter[1] * joined[1 : row_count + 1]
        + short_filter[2] * joined[:row_count]
    )


def rotary_turn(vectors, positions):
    half_dim = vectors.shape[-1] // 2
    frequency = rope_base ** (-jnp.arange(half_dim, dtype=jnp.float32) * 2.0 / vectors.shape[-1])
    angles = positions.astype(jnp.float32)[:, None] * frequency[None, :]
    cosine = jnp.cos(angles)[:, None, :]
    sine_part = jnp.sin(angles)[:, None, :]
    first_half = vectors[..., :half_dim]
    second = vectors[..., half_dim:]
    return jnp.concatenate(
        [first_half * cosine - second * sine_part, second * cosine + first_half * sine_part],
        axis=-1,
    )


def attend_tile(running, query_rows, query_pos, key_block, value_block, key_start):
    run_peak, denom, accumulated = running
    block_size = key_block.shape[0]
    score_scale = 1.0 / math.sqrt(key_block.shape[2])
    key_pos = key_start + jnp.arange(block_size, dtype=jnp.int32)
    scores = (
        jnp.einsum("shd,khd->hsk", query_rows, key_block, preferred_element_type=jnp.float32)
        * score_scale
    )
    allowed = (query_pos[:, None] >= key_pos[None, :])[None]
    masked = jnp.where(allowed, scores, mask_fill)
    new_peak = jnp.maximum(run_peak, jnp.max(masked, axis=2))
    weights = jnp.where(allowed, jnp.exp(masked - new_peak[:, :, None]), 0.0)
    factor = jnp.exp(run_peak - new_peak)
    denom = denom * factor + jnp.sum(weights, axis=2)
    accumulated = accumulated * factor[:, :, None] + jnp.einsum(
        "hsk,khd->hsd",
        weights.astype(jnp.bfloat16),
        value_block,
        preferred_element_type=jnp.float32,
    )
    return (new_peak, denom, accumulated)


def empty_state(head_count, rows):
    return (
        jnp.full((head_count, rows), mask_fill, jnp.float32),
        jnp.zeros((head_count, rows), jnp.float32),
        jnp.zeros((head_count, rows, HEAD_DIM), jnp.float32),
    )


def finish_rows(state):
    run_peak, denom, accumulated = state
    heads_out = accumulated / denom[:, :, None]
    rows = heads_out.shape[1]
    return (
        heads_out.transpose(1, 0, 2)
        .reshape(rows, heads_out.shape[0] * heads_out.shape[2])
        .astype(jnp.bfloat16)
    )


def per_device(resid_in, feats, short_filter, residues, rates, out_weight, norm_gain, attn_weight):
    row_count, chan_count = resid_in.shape
    width_all = out_weight.shape[1]
    short_out = short_mix(feats, short_filter)
    product = (short_out[:, 1] * short_out[:, 2]).astype(jnp.bfloat16)
    signal = product.T.astype(jnp.float32)
    lag_steps = jnp.arange(row_count, dtype=jnp.float32)
    tail_powers = jnp.exp(-rates[:, :, None] * (row_count - lag_steps))
    end_state = jnp.einsum("ct,cmt->cm", signal, tail_powers, precision=highest)
    gathered_states = gather_by_exchange(end_state, "ctx", concat_axis=0)
    shard_steps = jnp.arange(lax.axis_size("ctx"), dtype=jnp.float32)
    gap_count = lax.axis_index("ctx").astype(jnp.float32) - 1.0 - shard_steps
    decay = jnp.where(
        (gap_count >= 0.0)[:, None, None],
        jnp.exp(-rates[None] * row_count * jnp.maximum(gap_count, 0.0)[:, None, None]),
        0.0,
    )
    start_state = jnp.sum(decay * gathered_states, axis=0)
    conv_out = modal_conv(signal, residues, rates, start_state, block_limit=16).T
    gated = (short_out[:, 0] * conv_out).astype(jnp.bfloat16)
    tp_count = lax.axis_size("tp")
    partials = lax.dot_general(
        out_weight, gated, (((0,), (1,)), ((), ())), preferred_element_type=jnp.float32
    ).astype(jnp.bfloat16)
    received = lax.all_to_all(partials, "tp", split_axis=0, concat_axis=0, tiled=True)
    own_share = jnp.sum(
        received.reshape(tp_count, chan_count, row_count).astype(jnp.float32), axis=0
    )
    hyena_out = (resid_in.astype(jnp.float32) + own_share.T).astype(jnp.bfloat16)
    full_rows = gather_by_exchange(hyena_out, "tp").reshape(row_count, width_all)
    wide = full_rows.astype(jnp.float32)
    mean_square = jnp.mean(wide * wide, axis=1, keepdims=True)
    normed = (wide * lax.rsqrt(mean_square + eps_norm) * norm_gain).astype(jnp.bfloat16)
    projected = jnp.dot(
        normed, attn_weight.reshape(width_all, 3 * chan_count), preferred_element_type=jnp.float32
    ).reshape(row_count, 3, chan_count)
    head_count = chan_count // HEAD_DIM
    ctx_index = lax.axis_index("ctx")
    first_pos = ctx_index * row_count
    positions = first_pos + jnp.arange(row_count, dtype=jnp.int32)
    queries = rotary_turn(
        projected[:, 0].reshape(row_count, head_count, HEAD_DIM), positions
    ).astype(jnp.bfloat16)
    keys_all = rotary_turn(
        projected[:, 1].reshape(row_count, head_count, HEAD_DIM), positions
    ).astype(jnp.bfloat16)
    values = projected[:, 2].astype(jnp.bfloat16)
    key_pieces = (keys_all.reshape(row_count, chan_count), values)
    initial = empty_state(head_count, row_count)
    joined_kv = jnp.concatenate(key_pieces, axis=1)
    gathered_kv = gather_by_exchange(joined_kv, "ctx", concat_axis=0)
    gathered_kv = gathered_kv.reshape(lax.axis_size("ctx") * row_count, 2 * chan_count)
    key_rows = gathered_kv[:, :chan_count]
    value_rows = gathered_kv[:, chan_count:]
    key_total = key_rows.shape[0]
    tiles_block_size = math.gcd(key_total, 1024)
    block_count = key_total // tiles_block_size
    key_blocks = key_rows.reshape(block_count, tiles_block_size, head_count, HEAD_DIM)
    value_blocks = value_rows.reshape(block_count, tiles_block_size, head_count, HEAD_DIM)
    key_blocks, value_blocks, block_ids, block_size = (
        key_blocks,
        value_blocks,
        jnp.arange(block_count, dtype=jnp.int32),
        tiles_block_size,
    )

    def one_tile(carried, slot_item):
        key_block, value_block, block_index = slot_item
        key_start = block_index * block_size
        updated = attend_tile(carried, queries, positions, key_block, value_block, key_start)
        return (updated, None)

    result, _ = lax.scan(one_tile, initial, (key_blocks, value_blocks, block_ids))
    context = finish_rows(result)
    return (hyena_out, context)


def solution(mesh):
    in_specs = (
        P("ctx", "tp"),
        P("ctx", None, "tp"),
        P(None, None, "tp"),
        P("tp", None),
        P("tp", None),
        P("tp", None),
        P(),
        P(None, None, "tp"),
    )
    out_specs = (P("ctx", "tp"), P("ctx", "tp"))
    return jax.shard_map(
        per_device, mesh=mesh, in_specs=in_specs, out_specs=out_specs, check_vma=False
    )
```

```python
import math

import jax
import jax.numpy as jnp
from jax import lax
from jax.sharding import PartitionSpec as P

HEAD_DIM = 128


eps_norm = 1e-05
rope_base = 10000.0
mask_fill = -1e30
highest = lax.Precision.HIGHEST


def gather_by_exchange(block, axis, concat_axis=1):
    count = lax.axis_size(axis)
    copies = jnp.broadcast_to(block[None], (count,) + block.shape)
    return lax.all_to_all(copies, axis, split_axis=0, concat_axis=concat_axis, tiled=False)


def toeplitz_lower(filter_taps):
    chan_count, block_size = filter_taps.shape
    padded = jnp.concatenate(
        [jnp.zeros((chan_count, block_size - 1), jnp.float32), filter_taps], axis=1
    )
    flipped = padded[:, ::-1]
    tiled = jnp.tile(flipped, (1, block_size))
    offset = block_size - 1
    window = tiled[:, offset : offset + block_size * (2 * block_size - 2)]
    return window.reshape(chan_count, block_size, 2 * block_size - 2)[:, :, :block_size]


def modal_conv(signal, residues, rates, start_state, block_limit=128):
    chan_count, length = signal.shape
    block_size = math.gcd(length, block_limit)
    block_count = length // block_size
    weight = residues * jnp.sqrt(1.0 - jnp.exp(-2.0 * rates))
    lag_steps = jnp.arange(block_size, dtype=jnp.float32)
    powers = jnp.exp(-rates[:, :, None] * lag_steps)
    filter_taps = jnp.sum(weight[:, :, None] * powers, axis=1)
    toeplitz = toeplitz_lower(filter_taps)
    blocks = signal.reshape(chan_count, block_count, block_size)
    inner_part = jnp.einsum("cij,cnj->cni", toeplitz, blocks, precision=highest)
    tail_powers = jnp.exp(-rates[:, :, None] * (block_size - lag_steps))
    end_states = jnp.einsum("cnj,cmj->cnm", blocks, tail_powers, precision=highest)
    block_steps = jnp.arange(block_count, dtype=jnp.float32)
    gap_count = block_steps[:, None] - 1.0 - block_steps[None, :]
    live_mask = gap_count >= 0.0
    carry_mat = jnp.where(
        live_mask, jnp.exp(-rates[:, :, None, None] * block_size * jnp.maximum(gap_count, 0.0)), 0.0
    )
    states = jnp.einsum("cmnk,ckm->cnm", carry_mat, end_states, precision=highest)
    states = (
        states
        + jnp.exp(-rates[:, None, :] * block_size * block_steps[None, :, None])
        * start_state[:, None, :]
    )
    cross_part = jnp.einsum("cnm,cmi->cni", states * weight[:, None, :], powers, precision=highest)
    return (inner_part + cross_part).reshape(chan_count, length)


def short_conv(joined, short_filter):
    row_count = joined.shape[0] - 2
    return (
        short_filter[0] * joined[2:]
        + short_filter[1] * joined[1 : row_count + 1]
        + short_filter[2] * joined[:row_count]
    )


def rotary_turn(vectors, positions):
    half_dim = vectors.shape[-1] // 2
    frequency = rope_base ** (-jnp.arange(half_dim, dtype=jnp.float32) * 2.0 / vectors.shape[-1])
    angles = positions.astype(jnp.float32)[:, None] * frequency[None, :]
    cosine = jnp.cos(angles)[:, None, :]
    sine_part = jnp.sin(angles)[:, None, :]
    first_half = vectors[..., :half_dim]
    second = vectors[..., half_dim:]
    return jnp.concatenate(
        [first_half * cosine - second * sine_part, second * cosine + first_half * sine_part],
        axis=-1,
    )


def per_device(resid_in, feats, short_filter, residues, rates, out_weight, norm_gain, attn_weight):
    row_count, chan_count = resid_in.shape
    width_all = out_weight.shape[1]
    feats_wide = feats.astype(jnp.float32)
    ctx_count = lax.axis_size("ctx")
    ctx_index = lax.axis_index("ctx")
    lag_steps = jnp.arange(row_count, dtype=jnp.float32)
    tail_powers = jnp.exp(-rates[:, :, None] * (row_count - lag_steps))
    no_prior = jnp.zeros((2,) + feats_wide.shape[1:], jnp.float32)
    blind = short_conv(jnp.concatenate([no_prior, feats_wide], axis=0), short_filter)
    blind_product = (blind[:, 1] * blind[:, 2]).astype(jnp.bfloat16).T.astype(jnp.float32)
    late_state = jnp.einsum(
        "ct,cmt->cm", blind_product[:, 2:], tail_powers[:, :, 2:], precision=highest
    )
    mode_count = late_state.shape[1]
    head_rows = feats_wide[:2, 1:, :].reshape(4, chan_count).T
    tail_rows = feats_wide[-2:].reshape(6, chan_count).T
    payload = jnp.concatenate([late_state, head_rows, tail_rows], axis=1)
    received = gather_by_exchange(payload, "ctx", concat_axis=0)
    late_all = received[:, :, :mode_count]
    head_all = received[:, :, mode_count : mode_count + 4].reshape(ctx_count, chan_count, 2, 2)
    head_all = head_all.transpose(0, 2, 3, 1)
    tail_all = received[:, :, mode_count + 4 :].reshape(ctx_count, chan_count, 2, 3)
    tail_all = tail_all.transpose(0, 2, 3, 1)
    prev_tail = jnp.concatenate([jnp.zeros_like(tail_all[:1]), tail_all[:-1]], axis=0)
    edge_joined = jnp.concatenate([prev_tail[:, :, 1:], head_all], axis=1)
    taps = short_filter[:, 1:, :]
    edge_short = taps[0] * edge_joined[:, 2:] + taps[1] * edge_joined[:, 1:3] + taps[2] * edge_joined[:, :2]
    edge_product = (edge_short[:, :, 0] * edge_short[:, :, 1]).astype(jnp.bfloat16).astype(jnp.float32)
    gathered_states = (
        late_all
        + edge_product[:, 0, :, None] * tail_powers[None, :, :, 0]
        + edge_product[:, 1, :, None] * tail_powers[None, :, :, 1]
    )
    own_prior = lax.dynamic_index_in_dim(prev_tail, ctx_index, 0, keepdims=False)
    short_out = short_conv(jnp.concatenate([own_prior, feats_wide], axis=0), short_filter)
    product = (short_out[:, 1] * short_out[:, 2]).astype(jnp.bfloat16)
    signal = product.T.astype(jnp.float32)
    shard_steps = jnp.arange(ctx_count, dtype=jnp.float32)
    gap_count = ctx_index.astype(jnp.float32) - 1.0 - shard_steps
    decay = jnp.where(
        (gap_count >= 0.0)[:, None, None],
        jnp.exp(-rates[None] * row_count * jnp.maximum(gap_count, 0.0)[:, None, None]),
        0.0,
    )
    start_state = jnp.sum(decay * gathered_states, axis=0)
    conv_out = modal_conv(signal, residues, rates, start_state, block_limit=16).T
    gated = (short_out[:, 0] * conv_out).astype(jnp.bfloat16)
    tp_count = lax.axis_size("tp")
    partials = lax.dot_general(
        out_weight, gated, (((0,), (1,)), ((), ())), preferred_element_type=jnp.float32
    ).astype(jnp.bfloat16)
    received = lax.all_to_all(partials, "tp", split_axis=0, concat_axis=0, tiled=True)
    own_share = jnp.sum(
        received.reshape(tp_count, chan_count, row_count).astype(jnp.float32), axis=0
    )
    hyena_out = (resid_in.astype(jnp.float32) + own_share.T).astype(jnp.bfloat16)
    full_rows = gather_by_exchange(hyena_out, "tp").reshape(row_count, width_all)
    wide = full_rows.astype(jnp.float32)
    mean_square = jnp.mean(wide * wide, axis=1, keepdims=True)
    normed = (wide * lax.rsqrt(mean_square + eps_norm) * norm_gain).astype(jnp.bfloat16)
    projected = jnp.dot(
        normed, attn_weight.reshape(width_all, 3 * chan_count), preferred_element_type=jnp.float32
    ).reshape(row_count, 3, chan_count)
    head_count = chan_count // HEAD_DIM
    first_pos = ctx_index * row_count
    positions = first_pos + jnp.arange(row_count, dtype=jnp.int32)
    queries = rotary_turn(
        projected[:, 0].reshape(row_count, head_count, HEAD_DIM), positions
    ).astype(jnp.bfloat16)
    keys_all = rotary_turn(
        projected[:, 1].reshape(row_count, head_count, HEAD_DIM), positions
    ).astype(jnp.bfloat16)
    values = projected[:, 2].astype(jnp.bfloat16)
    joined_kv = jnp.concatenate([keys_all.reshape(row_count, chan_count), values], axis=1)
    gathered_kv = gather_by_exchange(joined_kv, "ctx", concat_axis=0)
    gathered_kv = gathered_kv.reshape(ctx_count * row_count, 2 * chan_count)
    key_total = gathered_kv.shape[0]
    key_rows = gathered_kv[:, :chan_count].reshape(key_total, head_count, HEAD_DIM)
    value_rows = gathered_kv[:, chan_count:].reshape(key_total, head_count, HEAD_DIM)
    key_pos = jnp.arange(key_total, dtype=jnp.int32)
    scores = jnp.einsum(
        "shd,khd->hsk", queries, key_rows, preferred_element_type=jnp.float32
    ) * (1.0 / math.sqrt(HEAD_DIM))
    allowed = (positions[:, None] >= key_pos[None, :])[None]
    masked = jnp.where(allowed, scores, mask_fill)
    run_peak = jnp.max(masked, axis=2, keepdims=True)
    probs = jnp.where(allowed, jnp.exp(masked - run_peak), 0.0)
    denom = jnp.sum(probs, axis=2, keepdims=True)
    summed = jnp.einsum(
        "hsk,khd->hsd", probs.astype(jnp.bfloat16), value_rows, preferred_element_type=jnp.float32
    )
    heads_out = summed / denom
    context = heads_out.transpose(1, 0, 2).reshape(row_count, chan_count).astype(jnp.bfloat16)
    return (hyena_out, context)


def solution(mesh):
    in_specs = (
        P("ctx", "tp"),
        P("ctx", None, "tp"),
        P(None, None, "tp"),
        P("tp", None),
        P("tp", None),
        P("tp", None),
        P(),
        P(None, None, "tp"),
    )
    out_specs = (P("ctx", "tp"), P("ctx", "tp"))
    return jax.shard_map(
        per_device, mesh=mesh, in_specs=in_specs, out_specs=out_specs, check_vma=False
    )
```

```python
import math

import jax
import jax.numpy as jnp
from jax import lax
from jax.sharding import PartitionSpec as P

HEAD_DIM = 128


eps_norm = 1e-05
rope_base = 10000.0
mask_fill = -1e30
highest = lax.Precision.HIGHEST


def shifted(value, axis, steps):
    count = lax.axis_size(axis)
    initial, last = (max(0, -steps), min(count, count - steps))
    return lax.ppermute(value, axis, [(source, source + steps) for source in range(initial, last)])


def gather_by_exchange(block, axis, concat_axis=1):
    count = lax.axis_size(axis)
    copies = jnp.broadcast_to(block[None], (count,) + block.shape)
    return lax.all_to_all(copies, axis, split_axis=0, concat_axis=concat_axis, tiled=False)


def toeplitz_lower(filter_taps):
    chan_count, block_size = filter_taps.shape
    padded = jnp.concatenate(
        [jnp.zeros((chan_count, block_size - 1), jnp.float32), filter_taps], axis=1
    )
    flipped = padded[:, ::-1]
    tiled = jnp.tile(flipped, (1, block_size))
    offset = block_size - 1
    window = tiled[:, offset : offset + block_size * (2 * block_size - 2)]
    return window.reshape(chan_count, block_size, 2 * block_size - 2)[:, :, :block_size]


def modal_conv(signal, residues, rates, start_state, block_limit=128):
    chan_count, length = signal.shape
    block_size = math.gcd(length, block_limit)
    block_count = length // block_size
    weight = residues * jnp.sqrt(1.0 - jnp.exp(-2.0 * rates))
    lag_steps = jnp.arange(block_size, dtype=jnp.float32)
    powers = jnp.exp(-rates[:, :, None] * lag_steps)
    filter_taps = jnp.sum(weight[:, :, None] * powers, axis=1)
    toeplitz = toeplitz_lower(filter_taps)
    blocks = signal.reshape(chan_count, block_count, block_size)
    inner_part = jnp.einsum("cij,cnj->cni", toeplitz, blocks, precision=highest)
    tail_powers = jnp.exp(-rates[:, :, None] * (block_size - lag_steps))
    end_states = jnp.einsum("cnj,cmj->cnm", blocks, tail_powers, precision=highest)
    block_steps = jnp.arange(block_count, dtype=jnp.float32)
    gap_count = block_steps[:, None] - 1.0 - block_steps[None, :]
    live_mask = gap_count >= 0.0
    carry_mat = jnp.where(
        live_mask, jnp.exp(-rates[:, :, None, None] * block_size * jnp.maximum(gap_count, 0.0)), 0.0
    )
    states = jnp.einsum("cmnk,ckm->cnm", carry_mat, end_states, precision=highest)
    states = (
        states
        + jnp.exp(-rates[:, None, :] * block_size * block_steps[None, :, None])
        * start_state[:, None, :]
    )
    cross_part = jnp.einsum("cnm,cmi->cni", states * weight[:, None, :], powers, precision=highest)
    return (inner_part + cross_part).reshape(chan_count, length)


def short_conv(joined, short_filter):
    row_count = joined.shape[0] - 2
    return (
        short_filter[0] * joined[2:]
        + short_filter[1] * joined[1 : row_count + 1]
        + short_filter[2] * joined[:row_count]
    )


def rotary_turn(vectors, positions):
    half_dim = vectors.shape[-1] // 2
    frequency = rope_base ** (-jnp.arange(half_dim, dtype=jnp.float32) * 2.0 / vectors.shape[-1])
    angles = positions.astype(jnp.float32)[:, None] * frequency[None, :]
    cosine = jnp.cos(angles)[:, None, :]
    sine_part = jnp.sin(angles)[:, None, :]
    first_half = vectors[..., :half_dim]
    second = vectors[..., half_dim:]
    return jnp.concatenate(
        [first_half * cosine - second * sine_part, second * cosine + first_half * sine_part],
        axis=-1,
    )


def per_device(resid_in, feats, short_filter, residues, rates, out_weight, norm_gain, attn_weight):
    row_count, chan_count = resid_in.shape
    width_all = out_weight.shape[1]
    feats_wide = feats.astype(jnp.float32)
    ctx_count = lax.axis_size("ctx")
    ctx_index = lax.axis_index("ctx")
    lag_steps = jnp.arange(row_count, dtype=jnp.float32)
    tail_powers = jnp.exp(-rates[:, :, None] * (row_count - lag_steps))
    no_prior = jnp.zeros((2,) + feats_wide.shape[1:], jnp.float32)
    blind = short_conv(jnp.concatenate([no_prior, feats_wide], axis=0), short_filter)
    blind_product = (blind[:, 1] * blind[:, 2]).astype(jnp.bfloat16).T.astype(jnp.float32)
    late_state = jnp.einsum(
        "ct,cmt->cm", blind_product[:, 2:], tail_powers[:, :, 2:], precision=highest
    )
    mode_count = late_state.shape[1]
    head_rows = feats_wide[:2, 1:, :].reshape(4, chan_count).T
    tail_rows = feats_wide[-2:].reshape(6, chan_count).T
    payload = jnp.concatenate([late_state, head_rows, tail_rows], axis=1)
    received = gather_by_exchange(payload, "ctx", concat_axis=0)
    late_all = received[:, :, :mode_count]
    head_all = received[:, :, mode_count : mode_count + 4].reshape(ctx_count, chan_count, 2, 2)
    head_all = head_all.transpose(0, 2, 3, 1)
    tail_all = received[:, :, mode_count + 4 :].reshape(ctx_count, chan_count, 2, 3)
    tail_all = tail_all.transpose(0, 2, 3, 1)
    prev_tail = jnp.concatenate([jnp.zeros_like(tail_all[:1]), tail_all[:-1]], axis=0)
    edge_joined = jnp.concatenate([prev_tail[:, :, 1:], head_all], axis=1)
    taps = short_filter[:, 1:, :]
    edge_short = taps[0] * edge_joined[:, 2:] + taps[1] * edge_joined[:, 1:3] + taps[2] * edge_joined[:, :2]
    edge_product = (edge_short[:, :, 0] * edge_short[:, :, 1]).astype(jnp.bfloat16).astype(jnp.float32)
    gathered_states = (
        late_all
        + edge_product[:, 0, :, None] * tail_powers[None, :, :, 0]
        + edge_product[:, 1, :, None] * tail_powers[None, :, :, 1]
    )
    own_prior = shifted(feats_wide[-2:], "ctx", 1)
    short_out = short_conv(jnp.concatenate([own_prior, feats_wide], axis=0), short_filter)
    product = (short_out[:, 1] * short_out[:, 2]).astype(jnp.bfloat16)
    signal = product.T.astype(jnp.float32)
    shard_steps = jnp.arange(ctx_count, dtype=jnp.float32)
    gap_count = ctx_index.astype(jnp.float32) - 1.0 - shard_steps
    decay = jnp.where(
        (gap_count >= 0.0)[:, None, None],
        jnp.exp(-rates[None] * row_count * jnp.maximum(gap_count, 0.0)[:, None, None]),
        0.0,
    )
    start_state = jnp.sum(decay * gathered_states, axis=0)
    conv_out = modal_conv(signal, residues, rates, start_state, block_limit=16).T
    gated = (short_out[:, 0] * conv_out).astype(jnp.bfloat16)
    tp_count = lax.axis_size("tp")
    partials = lax.dot_general(
        out_weight, gated, (((0,), (1,)), ((), ())), preferred_element_type=jnp.float32
    ).reshape(tp_count // 2, 2, chan_count, row_count)
    core = lax.axis_index("tp") % 2
    kept = lax.dynamic_index_in_dim(partials, core, 1, keepdims=False)
    given = lax.dynamic_index_in_dim(partials, 1 - core, 1, keepdims=False)
    from_sibling = lax.ppermute(
        given.astype(jnp.bfloat16), "tp", [(i, i ^ 1) for i in range(tp_count)]
    )
    chip_sum = (kept + from_sibling.astype(jnp.float32)).astype(jnp.bfloat16)
    same_core = [[2 * i + c for i in range(tp_count // 2)] for c in range(2)]
    received = lax.all_to_all(
        chip_sum, "tp", split_axis=0, concat_axis=0, axis_index_groups=same_core
    )
    own_share = jnp.sum(received.astype(jnp.float32), axis=0)
    hyena_out = (resid_in.astype(jnp.float32) + own_share.T).astype(jnp.bfloat16)
    full_rows = gather_by_exchange(hyena_out, "tp").reshape(row_count, width_all)
    wide = full_rows.astype(jnp.float32)
    mean_square = jnp.mean(wide * wide, axis=1, keepdims=True)
    normed = (wide * lax.rsqrt(mean_square + eps_norm) * norm_gain).astype(jnp.bfloat16)
    projected = jnp.dot(
        normed, attn_weight.reshape(width_all, 3 * chan_count), preferred_element_type=jnp.float32
    ).reshape(row_count, 3, chan_count)
    head_count = chan_count // HEAD_DIM
    first_pos = ctx_index * row_count
    positions = first_pos + jnp.arange(row_count, dtype=jnp.int32)
    queries = rotary_turn(
        projected[:, 0].reshape(row_count, head_count, HEAD_DIM), positions
    ).astype(jnp.bfloat16)
    keys_all = rotary_turn(
        projected[:, 1].reshape(row_count, head_count, HEAD_DIM), positions
    ).astype(jnp.bfloat16)
    values = projected[:, 2].astype(jnp.bfloat16)
    joined_kv = jnp.concatenate([keys_all.reshape(row_count, chan_count), values], axis=1)
    gathered_kv = gather_by_exchange(joined_kv, "ctx", concat_axis=0)
    gathered_kv = gathered_kv.reshape(ctx_count * row_count, 2 * chan_count)
    key_total = gathered_kv.shape[0]
    key_rows = gathered_kv[:, :chan_count].reshape(key_total, head_count, HEAD_DIM)
    value_rows = gathered_kv[:, chan_count:].reshape(key_total, head_count, HEAD_DIM)
    key_pos = jnp.arange(key_total, dtype=jnp.int32)
    scores = jnp.einsum(
        "shd,khd->hsk", queries, key_rows, preferred_element_type=jnp.float32
    ) * (1.0 / math.sqrt(HEAD_DIM))
    allowed = (positions[:, None] >= key_pos[None, :])[None]
    masked = jnp.where(allowed, scores, mask_fill)
    run_peak = jnp.max(masked, axis=2, keepdims=True)
    probs = jnp.where(allowed, jnp.exp(masked - run_peak), 0.0)
    denom = jnp.sum(probs, axis=2, keepdims=True)
    summed = jnp.einsum(
        "hsk,khd->hsd", probs.astype(jnp.bfloat16), value_rows, preferred_element_type=jnp.float32
    )
    heads_out = summed / denom
    context = heads_out.transpose(1, 0, 2).reshape(row_count, chan_count).astype(jnp.bfloat16)
    return (hyena_out, context)


def solution(mesh):
    in_specs = (
        P("ctx", "tp"),
        P("ctx", None, "tp"),
        P(None, None, "tp"),
        P("tp", None),
        P("tp", None),
        P("tp", None),
        P(),
        P(None, None, "tp"),
    )
    out_specs = (P("ctx", "tp"), P("ctx", "tp"))
    return jax.shard_map(
        per_device, mesh=mesh, in_specs=in_specs, out_specs=out_specs, check_vma=False
    )
```

```python
import math

import jax
import jax.numpy as jnp
from jax import lax
from jax.sharding import PartitionSpec as P

HEAD_DIM = 128


eps_norm = 1e-05
rope_base = 10000.0
mask_fill = -1e30
highest = lax.Precision.HIGHEST


def gather_by_exchange(block, axis, concat_axis=1):
    count = lax.axis_size(axis)
    copies = jnp.broadcast_to(block[None], (count,) + block.shape)
    return lax.all_to_all(copies, axis, split_axis=0, concat_axis=concat_axis, tiled=False)


def toeplitz_lower(filter_taps):
    chan_count, block_size = filter_taps.shape
    padded = jnp.concatenate(
        [jnp.zeros((chan_count, block_size - 1), jnp.float32), filter_taps], axis=1
    )
    flipped = padded[:, ::-1]
    tiled = jnp.tile(flipped, (1, block_size))
    offset = block_size - 1
    window = tiled[:, offset : offset + block_size * (2 * block_size - 2)]
    return window.reshape(chan_count, block_size, 2 * block_size - 2)[:, :, :block_size]


def modal_conv(signal, residues, rates, start_state, block_limit=128):
    chan_count, length = signal.shape
    block_size = math.gcd(length, block_limit)
    block_count = length // block_size
    weight = residues * jnp.sqrt(1.0 - jnp.exp(-2.0 * rates))
    lag_steps = jnp.arange(block_size, dtype=jnp.float32)
    powers = jnp.exp(-rates[:, :, None] * lag_steps)
    filter_taps = jnp.sum(weight[:, :, None] * powers, axis=1)
    toeplitz = toeplitz_lower(filter_taps)
    blocks = signal.reshape(chan_count, block_count, block_size)
    inner_part = jnp.einsum("cij,cnj->cni", toeplitz, blocks, precision=highest)
    tail_powers = jnp.exp(-rates[:, :, None] * (block_size - lag_steps))
    end_states = jnp.einsum("cnj,cmj->cnm", blocks, tail_powers, precision=highest)
    block_steps = jnp.arange(block_count, dtype=jnp.float32)
    gap_count = block_steps[:, None] - 1.0 - block_steps[None, :]
    live_mask = gap_count >= 0.0
    carry_mat = jnp.where(
        live_mask, jnp.exp(-rates[:, :, None, None] * block_size * jnp.maximum(gap_count, 0.0)), 0.0
    )
    states = jnp.einsum("cmnk,ckm->cnm", carry_mat, end_states, precision=highest)
    states = (
        states
        + jnp.exp(-rates[:, None, :] * block_size * block_steps[None, :, None])
        * start_state[:, None, :]
    )
    cross_part = jnp.einsum("cnm,cmi->cni", states * weight[:, None, :], powers, precision=highest)
    return (inner_part + cross_part).reshape(chan_count, length)


def short_conv(joined, short_filter):
    row_count = joined.shape[0] - 2
    return (
        short_filter[0] * joined[2:]
        + short_filter[1] * joined[1 : row_count + 1]
        + short_filter[2] * joined[:row_count]
    )


def rotary_turn(vectors, positions):
    half_dim = vectors.shape[-1] // 2
    frequency = rope_base ** (-jnp.arange(half_dim, dtype=jnp.float32) * 2.0 / vectors.shape[-1])
    angles = positions.astype(jnp.float32)[:, None] * frequency[None, :]
    cosine = jnp.cos(angles)[:, None, :]
    sine_part = jnp.sin(angles)[:, None, :]
    first_half = vectors[..., :half_dim]
    second = vectors[..., half_dim:]
    return jnp.concatenate(
        [first_half * cosine - second * sine_part, second * cosine + first_half * sine_part],
        axis=-1,
    )


def per_device(resid_in, feats, short_filter, residues, rates, out_weight, norm_gain, attn_weight):
    row_count, chan_count = resid_in.shape
    width_all = out_weight.shape[1]
    feats_wide = feats.astype(jnp.float32)
    ctx_count = lax.axis_size("ctx")
    ctx_index = lax.axis_index("ctx")
    lag_steps = jnp.arange(row_count, dtype=jnp.float32)
    tail_powers = jnp.exp(-rates[:, :, None] * (row_count - lag_steps))
    no_prior = jnp.zeros((2,) + feats_wide.shape[1:], jnp.float32)
    blind = short_conv(jnp.concatenate([no_prior, feats_wide], axis=0), short_filter)
    blind_product = (blind[:, 1] * blind[:, 2]).astype(jnp.bfloat16).T.astype(jnp.float32)
    late_state = jnp.einsum(
        "ct,cmt->cm", blind_product[:, 2:], tail_powers[:, :, 2:], precision=highest
    )
    mode_count = late_state.shape[1]
    head_rows = feats_wide[:2, 1:, :].reshape(4, chan_count).T
    tail_rows = feats_wide[-2:].reshape(6, chan_count).T
    payload = jnp.concatenate([late_state, head_rows, tail_rows], axis=1)
    received = gather_by_exchange(payload, "ctx", concat_axis=0)
    late_all = received[:, :, :mode_count]
    head_all = received[:, :, mode_count : mode_count + 4].reshape(ctx_count, chan_count, 2, 2)
    head_all = head_all.transpose(0, 2, 3, 1)
    tail_all = received[:, :, mode_count + 4 :].reshape(ctx_count, chan_count, 2, 3)
    tail_all = tail_all.transpose(0, 2, 3, 1)
    prev_tail = jnp.concatenate([jnp.zeros_like(tail_all[:1]), tail_all[:-1]], axis=0)
    edge_joined = jnp.concatenate([prev_tail[:, :, 1:], head_all], axis=1)
    taps = short_filter[:, 1:, :]
    edge_short = taps[0] * edge_joined[:, 2:] + taps[1] * edge_joined[:, 1:3] + taps[2] * edge_joined[:, :2]
    edge_product = (edge_short[:, :, 0] * edge_short[:, :, 1]).astype(jnp.bfloat16).astype(jnp.float32)
    gathered_states = (
        late_all
        + edge_product[:, 0, :, None] * tail_powers[None, :, :, 0]
        + edge_product[:, 1, :, None] * tail_powers[None, :, :, 1]
    )
    shard_steps = jnp.arange(ctx_count, dtype=jnp.float32)
    gap_count = ctx_index.astype(jnp.float32) - 1.0 - shard_steps
    decay = jnp.where(
        (gap_count >= 0.0)[:, None, None],
        jnp.exp(-rates[None] * row_count * jnp.maximum(gap_count, 0.0)[:, None, None]),
        0.0,
    )
    start_state = jnp.sum(decay * gathered_states, axis=0)
    conv_blind = modal_conv(
        blind_product, residues, rates, jnp.zeros_like(rates), block_limit=16
    )
    weight = residues * jnp.sqrt(1.0 - jnp.exp(-2.0 * rates))
    full_powers = jnp.exp(-rates[:, :, None] * lag_steps)
    long_taps = jnp.sum(weight[:, :, None] * full_powers, axis=1)
    later_taps = jnp.concatenate([jnp.zeros_like(long_taps[:, :1]), long_taps[:, :-1]], axis=1)
    own_prior = lax.dynamic_index_in_dim(prev_tail, ctx_index, 0, keepdims=False)
    own_edge = short_conv(jnp.concatenate([own_prior, feats_wide[:2]], axis=0), short_filter)
    own_edge_product = (own_edge[:, 1] * own_edge[:, 2]).astype(jnp.bfloat16).astype(jnp.float32)
    delta = own_edge_product - blind_product[:, :2].T
    start_part = jnp.sum((weight * start_state)[:, :, None] * full_powers, axis=1)
    conv_out = (
        conv_blind + start_part + long_taps * delta[0][:, None] + later_taps * delta[1][:, None]
    ).T
    short_query = jnp.concatenate([own_edge[:, 0], blind[2:, 0]], axis=0)
    gated = (short_query * conv_out).astype(jnp.bfloat16)
    tp_count = lax.axis_size("tp")
    partials = lax.dot_general(
        out_weight, gated, (((0,), (1,)), ((), ())), preferred_element_type=jnp.float32
    ).astype(jnp.bfloat16)
    received = lax.all_to_all(partials, "tp", split_axis=0, concat_axis=0, tiled=True)
    own_share = jnp.sum(
        received.reshape(tp_count, chan_count, row_count).astype(jnp.float32), axis=0
    )
    hyena_out = (resid_in.astype(jnp.float32) + own_share.T).astype(jnp.bfloat16)
    full_rows = gather_by_exchange(hyena_out, "tp").reshape(row_count, width_all)
    wide = full_rows.astype(jnp.float32)
    mean_square = jnp.mean(wide * wide, axis=1, keepdims=True)
    normed = (wide * lax.rsqrt(mean_square + eps_norm) * norm_gain).astype(jnp.bfloat16)
    projected = jnp.dot(
        normed, attn_weight.reshape(width_all, 3 * chan_count), preferred_element_type=jnp.float32
    ).reshape(row_count, 3, chan_count)
    head_count = chan_count // HEAD_DIM
    first_pos = ctx_index * row_count
    positions = first_pos + jnp.arange(row_count, dtype=jnp.int32)
    queries = rotary_turn(
        projected[:, 0].reshape(row_count, head_count, HEAD_DIM), positions
    ).astype(jnp.bfloat16)
    keys_all = rotary_turn(
        projected[:, 1].reshape(row_count, head_count, HEAD_DIM), positions
    ).astype(jnp.bfloat16)
    values = projected[:, 2].astype(jnp.bfloat16)
    joined_kv = jnp.concatenate([keys_all.reshape(row_count, chan_count), values], axis=1)
    gathered_kv = gather_by_exchange(joined_kv, "ctx", concat_axis=0)
    gathered_kv = gathered_kv.reshape(ctx_count * row_count, 2 * chan_count)
    key_total = gathered_kv.shape[0]
    key_rows = gathered_kv[:, :chan_count].reshape(key_total, head_count, HEAD_DIM)
    value_rows = gathered_kv[:, chan_count:].reshape(key_total, head_count, HEAD_DIM)
    key_pos = jnp.arange(key_total, dtype=jnp.int32)
    scores = jnp.einsum(
        "shd,khd->hsk", queries, key_rows, preferred_element_type=jnp.float32
    ) * (1.0 / math.sqrt(HEAD_DIM))
    allowed = (positions[:, None] >= key_pos[None, :])[None]
    masked = jnp.where(allowed, scores, mask_fill)
    run_peak = jnp.max(masked, axis=2, keepdims=True)
    probs = jnp.where(allowed, jnp.exp(masked - run_peak), 0.0)
    denom = jnp.sum(probs, axis=2, keepdims=True)
    summed = jnp.einsum(
        "hsk,khd->hsd", probs.astype(jnp.bfloat16), value_rows, preferred_element_type=jnp.float32
    )
    heads_out = summed / denom
    context = heads_out.transpose(1, 0, 2).reshape(row_count, chan_count).astype(jnp.bfloat16)
    return (hyena_out, context)


def solution(mesh):
    in_specs = (
        P("ctx", "tp"),
        P("ctx", None, "tp"),
        P(None, None, "tp"),
        P("tp", None),
        P("tp", None),
        P("tp", None),
        P(),
        P(None, None, "tp"),
    )
    out_specs = (P("ctx", "tp"), P("ctx", "tp"))
    return jax.shard_map(
        per_device, mesh=mesh, in_specs=in_specs, out_specs=out_specs, check_vma=False
    )
```

```python
import math

import jax
import jax.numpy as jnp
from jax import lax
from jax.sharding import PartitionSpec as P

HEAD_DIM = 128


eps_norm = 1e-05
rope_base = 10000.0
mask_fill = -1e30
highest = lax.Precision.HIGHEST


def gather_by_exchange(block, axis, concat_axis=1):
    count = lax.axis_size(axis)
    copies = jnp.broadcast_to(block[None], (count,) + block.shape)
    return lax.all_to_all(copies, axis, split_axis=0, concat_axis=concat_axis, tiled=False)


def toeplitz_lower(filter_taps):
    chan_count, block_size = filter_taps.shape
    padded = jnp.concatenate(
        [jnp.zeros((chan_count, block_size - 1), jnp.float32), filter_taps], axis=1
    )
    flipped = padded[:, ::-1]
    tiled = jnp.tile(flipped, (1, block_size))
    offset = block_size - 1
    window = tiled[:, offset : offset + block_size * (2 * block_size - 2)]
    return window.reshape(chan_count, block_size, 2 * block_size - 2)[:, :, :block_size]


def modal_conv(signal, residues, rates, start_state, block_limit=128):
    chan_count, length = signal.shape
    block_size = math.gcd(length, block_limit)
    block_count = length // block_size
    weight = residues * jnp.sqrt(1.0 - jnp.exp(-2.0 * rates))
    lag_steps = jnp.arange(block_size, dtype=jnp.float32)
    powers = jnp.exp(-rates[:, :, None] * lag_steps)
    filter_taps = jnp.sum(weight[:, :, None] * powers, axis=1)
    toeplitz = toeplitz_lower(filter_taps)
    blocks = signal.reshape(chan_count, block_count, block_size)
    inner_part = jnp.einsum("cij,cnj->cni", toeplitz, blocks, precision=highest)
    tail_powers = jnp.exp(-rates[:, :, None] * (block_size - lag_steps))
    end_states = jnp.einsum("cnj,cmj->cnm", blocks, tail_powers, precision=highest)
    block_steps = jnp.arange(block_count, dtype=jnp.float32)
    gap_count = block_steps[:, None] - 1.0 - block_steps[None, :]
    live_mask = gap_count >= 0.0
    carry_mat = jnp.where(
        live_mask, jnp.exp(-rates[:, :, None, None] * block_size * jnp.maximum(gap_count, 0.0)), 0.0
    )
    states = jnp.einsum("cmnk,ckm->cnm", carry_mat, end_states, precision=highest)
    states = (
        states
        + jnp.exp(-rates[:, None, :] * block_size * block_steps[None, :, None])
        * start_state[:, None, :]
    )
    cross_part = jnp.einsum("cnm,cmi->cni", states * weight[:, None, :], powers, precision=highest)
    return (inner_part + cross_part).reshape(chan_count, length)


def short_conv(joined, short_filter):
    row_count = joined.shape[0] - 2
    return (
        short_filter[0] * joined[2:]
        + short_filter[1] * joined[1 : row_count + 1]
        + short_filter[2] * joined[:row_count]
    )


def rotary_turn(vectors, positions):
    half_dim = vectors.shape[-1] // 2
    frequency = rope_base ** (-jnp.arange(half_dim, dtype=jnp.float32) * 2.0 / vectors.shape[-1])
    angles = positions.astype(jnp.float32)[:, None] * frequency[None, :]
    cosine = jnp.cos(angles)[:, None, :]
    sine_part = jnp.sin(angles)[:, None, :]
    first_half = vectors[..., :half_dim]
    second = vectors[..., half_dim:]
    return jnp.concatenate(
        [first_half * cosine - second * sine_part, second * cosine + first_half * sine_part],
        axis=-1,
    )


def per_device(resid_in, feats, short_filter, residues, rates, out_weight, norm_gain, attn_weight):
    row_count, chan_count = resid_in.shape
    width_all = out_weight.shape[1]
    feats_wide = feats.astype(jnp.float32)
    ctx_count = lax.axis_size("ctx")
    ctx_index = lax.axis_index("ctx")
    lag_steps = jnp.arange(row_count, dtype=jnp.float32)
    tail_powers = jnp.exp(-rates[:, :, None] * (row_count - lag_steps))
    no_prior = jnp.zeros((2,) + feats_wide.shape[1:], jnp.float32)
    blind = short_conv(jnp.concatenate([no_prior, feats_wide], axis=0), short_filter)
    blind_product = (blind[:, 1] * blind[:, 2]).astype(jnp.bfloat16).T.astype(jnp.float32)
    late_state = jnp.einsum(
        "ct,cmt->cm", blind_product[:, 2:], tail_powers[:, :, 2:], precision=highest
    )
    mode_count = late_state.shape[1]
    head_rows = feats_wide[:2, 1:, :].reshape(4, chan_count).T
    tail_rows = feats_wide[-2:].reshape(6, chan_count).T
    payload = jnp.concatenate([late_state, head_rows, tail_rows], axis=1)
    received = gather_by_exchange(payload, "ctx", concat_axis=0)
    late_all = received[:, :, :mode_count]
    head_all = received[:, :, mode_count : mode_count + 4].reshape(ctx_count, chan_count, 2, 2)
    head_all = head_all.transpose(0, 2, 3, 1)
    tail_all = received[:, :, mode_count + 4 :].reshape(ctx_count, chan_count, 2, 3)
    tail_all = tail_all.transpose(0, 2, 3, 1)
    prev_tail = jnp.concatenate([jnp.zeros_like(tail_all[:1]), tail_all[:-1]], axis=0)
    edge_joined = jnp.concatenate([prev_tail[:, :, 1:], head_all], axis=1)
    taps = short_filter[:, 1:, :]
    edge_short = taps[0] * edge_joined[:, 2:] + taps[1] * edge_joined[:, 1:3] + taps[2] * edge_joined[:, :2]
    edge_product = (edge_short[:, :, 0] * edge_short[:, :, 1]).astype(jnp.bfloat16).astype(jnp.float32)
    gathered_states = (
        late_all
        + edge_product[:, 0, :, None] * tail_powers[None, :, :, 0]
        + edge_product[:, 1, :, None] * tail_powers[None, :, :, 1]
    )
    shard_steps = jnp.arange(ctx_count, dtype=jnp.float32)
    gap_count = ctx_index.astype(jnp.float32) - 1.0 - shard_steps
    decay = jnp.where(
        (gap_count >= 0.0)[:, None, None],
        jnp.exp(-rates[None] * row_count * jnp.maximum(gap_count, 0.0)[:, None, None]),
        0.0,
    )
    start_state = jnp.sum(decay * gathered_states, axis=0)
    conv_blind = modal_conv(
        blind_product, residues, rates, jnp.zeros_like(rates), block_limit=16
    )
    weight = residues * jnp.sqrt(1.0 - jnp.exp(-2.0 * rates))
    full_powers = jnp.exp(-rates[:, :, None] * lag_steps)
    long_taps = jnp.sum(weight[:, :, None] * full_powers, axis=1)
    later_taps = jnp.concatenate([jnp.zeros_like(long_taps[:, :1]), long_taps[:, :-1]], axis=1)
    own_prior = lax.dynamic_index_in_dim(prev_tail, ctx_index, 0, keepdims=False)
    own_edge = short_conv(jnp.concatenate([own_prior, feats_wide[:2]], axis=0), short_filter)
    own_edge_product = (own_edge[:, 1] * own_edge[:, 2]).astype(jnp.bfloat16).astype(jnp.float32)
    delta = own_edge_product - blind_product[:, :2].T
    start_part = jnp.sum((weight * start_state)[:, :, None] * full_powers, axis=1)
    conv_out = (
        conv_blind + start_part + long_taps * delta[0][:, None] + later_taps * delta[1][:, None]
    ).T
    short_query = jnp.concatenate([own_edge[:, 0], blind[2:, 0]], axis=0)
    gated = (short_query * conv_out).astype(jnp.bfloat16)
    tp_count = lax.axis_size("tp")
    pair_weight = out_weight.reshape(chan_count, tp_count // 2, 2, width_all // tp_count)
    even_part = jnp.einsum(
        "tc,cid->itd", gated, pair_weight[:, :, 0], preferred_element_type=jnp.float32
    )
    odd_part = jnp.einsum(
        "tc,cid->itd", gated, pair_weight[:, :, 1], preferred_element_type=jnp.float32
    )
    is_even = lax.axis_index("tp") % 2 == 0
    kept = jnp.where(is_even, even_part, odd_part)
    given = jnp.where(is_even, odd_part, even_part).astype(jnp.bfloat16)
    from_sibling = lax.ppermute(given, "tp", [(i, i ^ 1) for i in range(tp_count)])
    chip_sum = (kept + from_sibling.astype(jnp.float32)).astype(jnp.bfloat16)
    same_core = [[2 * i + c for i in range(tp_count // 2)] for c in range(2)]
    received = lax.all_to_all(
        chip_sum, "tp", split_axis=0, concat_axis=0, axis_index_groups=same_core
    )
    own_share = jnp.sum(received.astype(jnp.float32), axis=0)
    hyena_out = (resid_in.astype(jnp.float32) + own_share).astype(jnp.bfloat16)
    full_rows = gather_by_exchange(hyena_out, "tp").reshape(row_count, width_all)
    wide = full_rows.astype(jnp.float32)
    mean_square = jnp.mean(wide * wide, axis=1, keepdims=True)
    normed = (wide * lax.rsqrt(mean_square + eps_norm) * norm_gain).astype(jnp.bfloat16)
    projected = jnp.dot(
        normed, attn_weight.reshape(width_all, 3 * chan_count), preferred_element_type=jnp.float32
    ).reshape(row_count, 3, chan_count)
    head_count = chan_count // HEAD_DIM
    first_pos = ctx_index * row_count
    positions = first_pos + jnp.arange(row_count, dtype=jnp.int32)
    queries = rotary_turn(
        projected[:, 0].reshape(row_count, head_count, HEAD_DIM), positions
    ).astype(jnp.bfloat16)
    keys_all = rotary_turn(
        projected[:, 1].reshape(row_count, head_count, HEAD_DIM), positions
    ).astype(jnp.bfloat16)
    values = projected[:, 2].astype(jnp.bfloat16)
    joined_kv = jnp.concatenate([keys_all.reshape(row_count, chan_count), values], axis=1)
    gathered_kv = gather_by_exchange(joined_kv, "ctx", concat_axis=0)
    gathered_kv = gathered_kv.reshape(ctx_count * row_count, 2 * chan_count)
    key_total = gathered_kv.shape[0]
    key_rows = gathered_kv[:, :chan_count].reshape(key_total, head_count, HEAD_DIM)
    value_rows = gathered_kv[:, chan_count:].reshape(key_total, head_count, HEAD_DIM)
    key_pos = jnp.arange(key_total, dtype=jnp.int32)
    scores = jnp.einsum(
        "shd,khd->hsk", queries, key_rows, preferred_element_type=jnp.float32
    ) * (1.0 / math.sqrt(HEAD_DIM))
    allowed = (positions[:, None] >= key_pos[None, :])[None]
    masked = jnp.where(allowed, scores, mask_fill)
    run_peak = jnp.max(masked, axis=2, keepdims=True)
    probs = jnp.where(allowed, jnp.exp(masked - run_peak), 0.0)
    denom = jnp.sum(probs, axis=2, keepdims=True)
    summed = jnp.einsum(
        "hsk,khd->hsd", probs.astype(jnp.bfloat16), value_rows, preferred_element_type=jnp.float32
    )
    heads_out = summed / denom
    context = heads_out.transpose(1, 0, 2).reshape(row_count, chan_count).astype(jnp.bfloat16)
    return (hyena_out, context)


def solution(mesh):
    in_specs = (
        P("ctx", "tp"),
        P("ctx", None, "tp"),
        P(None, None, "tp"),
        P("tp", None),
        P("tp", None),
        P("tp", None),
        P(),
        P(None, None, "tp"),
    )
    out_specs = (P("ctx", "tp"), P("ctx", "tp"))
    return jax.shard_map(
        per_device, mesh=mesh, in_specs=in_specs, out_specs=out_specs, check_vma=False
    )
```

```python
import math

import jax
import jax.numpy as jnp
from jax import lax
from jax.sharding import PartitionSpec as P

HEAD_DIM = 128


eps_norm = 1e-05
rope_base = 10000.0
mask_fill = -1e30
highest = lax.Precision.HIGHEST


def gather_by_exchange(block, axis, concat_axis=1):
    count = lax.axis_size(axis)
    copies = jnp.broadcast_to(block[None], (count,) + block.shape)
    return lax.all_to_all(copies, axis, split_axis=0, concat_axis=concat_axis, tiled=False)


def toeplitz_lower(filter_taps):
    chan_count, block_size = filter_taps.shape
    padded = jnp.concatenate(
        [jnp.zeros((chan_count, block_size - 1), jnp.float32), filter_taps], axis=1
    )
    flipped = padded[:, ::-1]
    tiled = jnp.tile(flipped, (1, block_size))
    offset = block_size - 1
    window = tiled[:, offset : offset + block_size * (2 * block_size - 2)]
    return window.reshape(chan_count, block_size, 2 * block_size - 2)[:, :, :block_size]


def modal_conv(signal, residues, rates, start_state, block_limit=128):
    chan_count, length = signal.shape
    block_size = math.gcd(length, block_limit)
    block_count = length // block_size
    weight = residues * jnp.sqrt(1.0 - jnp.exp(-2.0 * rates))
    lag_steps = jnp.arange(block_size, dtype=jnp.float32)
    powers = jnp.exp(-rates[:, :, None] * lag_steps)
    filter_taps = jnp.sum(weight[:, :, None] * powers, axis=1)
    toeplitz = toeplitz_lower(filter_taps)
    blocks = signal.reshape(chan_count, block_count, block_size)
    inner_part = jnp.einsum("cij,cnj->cni", toeplitz, blocks, precision=highest)
    tail_powers = jnp.exp(-rates[:, :, None] * (block_size - lag_steps))
    end_states = jnp.einsum("cnj,cmj->cnm", blocks, tail_powers, precision=highest)
    block_steps = jnp.arange(block_count, dtype=jnp.float32)
    gap_count = block_steps[:, None] - 1.0 - block_steps[None, :]
    live_mask = gap_count >= 0.0
    carry_mat = jnp.where(
        live_mask, jnp.exp(-rates[:, :, None, None] * block_size * jnp.maximum(gap_count, 0.0)), 0.0
    )
    states = jnp.einsum("cmnk,ckm->cnm", carry_mat, end_states, precision=highest)
    states = (
        states
        + jnp.exp(-rates[:, None, :] * block_size * block_steps[None, :, None])
        * start_state[:, None, :]
    )
    cross_part = jnp.einsum("cnm,cmi->cni", states * weight[:, None, :], powers, precision=highest)
    return (inner_part + cross_part).reshape(chan_count, length)


def short_conv(joined, short_filter):
    row_count = joined.shape[0] - 2
    return (
        short_filter[0] * joined[2:]
        + short_filter[1] * joined[1 : row_count + 1]
        + short_filter[2] * joined[:row_count]
    )


def rotary_turn(vectors, positions):
    half_dim = vectors.shape[-1] // 2
    frequency = rope_base ** (-jnp.arange(half_dim, dtype=jnp.float32) * 2.0 / vectors.shape[-1])
    angles = positions.astype(jnp.float32)[:, None] * frequency[None, :]
    cosine = jnp.cos(angles)[:, None, :]
    sine_part = jnp.sin(angles)[:, None, :]
    first_half = vectors[..., :half_dim]
    second = vectors[..., half_dim:]
    return jnp.concatenate(
        [first_half * cosine - second * sine_part, second * cosine + first_half * sine_part],
        axis=-1,
    )


def per_device(resid_in, feats, short_filter, residues, rates, out_weight, norm_gain, attn_weight):
    row_count, chan_count = resid_in.shape
    width_all = out_weight.shape[1]
    feats_wide = feats.astype(jnp.float32)
    ctx_count = lax.axis_size("ctx")
    ctx_index = lax.axis_index("ctx")
    lag_steps = jnp.arange(row_count, dtype=jnp.float32)
    tail_powers = jnp.exp(-rates[:, :, None] * (row_count - lag_steps))
    no_prior = jnp.zeros((2,) + feats_wide.shape[1:], jnp.float32)
    blind = short_conv(jnp.concatenate([no_prior, feats_wide], axis=0), short_filter)
    blind_product = (blind[:, 1] * blind[:, 2]).astype(jnp.bfloat16).T.astype(jnp.float32)
    late_state = jnp.einsum(
        "ct,cmt->cm", blind_product[:, 2:], tail_powers[:, :, 2:], precision=highest
    )
    mode_count = late_state.shape[1]
    head_rows = feats_wide[:2, 1:, :].reshape(4, chan_count).T
    tail_rows = feats_wide[-2:].reshape(6, chan_count).T
    payload = jnp.concatenate([late_state, head_rows, tail_rows], axis=1)
    received = gather_by_exchange(payload, "ctx", concat_axis=0)
    late_all = received[:, :, :mode_count]
    head_all = received[:, :, mode_count : mode_count + 4].reshape(ctx_count, chan_count, 2, 2)
    head_all = head_all.transpose(0, 2, 3, 1)
    tail_all = received[:, :, mode_count + 4 :].reshape(ctx_count, chan_count, 2, 3)
    tail_all = tail_all.transpose(0, 2, 3, 1)
    prev_tail = jnp.concatenate([jnp.zeros_like(tail_all[:1]), tail_all[:-1]], axis=0)
    edge_joined = jnp.concatenate([prev_tail[:, :, 1:], head_all], axis=1)
    taps = short_filter[:, 1:, :]
    edge_short = taps[0] * edge_joined[:, 2:] + taps[1] * edge_joined[:, 1:3] + taps[2] * edge_joined[:, :2]
    edge_product = (edge_short[:, :, 0] * edge_short[:, :, 1]).astype(jnp.bfloat16).astype(jnp.float32)
    gathered_states = (
        late_all
        + edge_product[:, 0, :, None] * tail_powers[None, :, :, 0]
        + edge_product[:, 1, :, None] * tail_powers[None, :, :, 1]
    )
    shard_steps = jnp.arange(ctx_count, dtype=jnp.float32)
    gap_count = ctx_index.astype(jnp.float32) - 1.0 - shard_steps
    decay = jnp.where(
        (gap_count >= 0.0)[:, None, None],
        jnp.exp(-rates[None] * row_count * jnp.maximum(gap_count, 0.0)[:, None, None]),
        0.0,
    )
    start_state = jnp.sum(decay * gathered_states, axis=0)
    conv_blind = modal_conv(
        blind_product, residues, rates, jnp.zeros_like(rates), block_limit=16
    )
    weight = residues * jnp.sqrt(1.0 - jnp.exp(-2.0 * rates))
    full_powers = jnp.exp(-rates[:, :, None] * lag_steps)
    long_taps = jnp.sum(weight[:, :, None] * full_powers, axis=1)
    later_taps = jnp.concatenate([jnp.zeros_like(long_taps[:, :1]), long_taps[:, :-1]], axis=1)
    own_prior = lax.dynamic_index_in_dim(prev_tail, ctx_index, 0, keepdims=False)
    own_edge = short_conv(jnp.concatenate([own_prior, feats_wide[:2]], axis=0), short_filter)
    own_edge_product = (own_edge[:, 1] * own_edge[:, 2]).astype(jnp.bfloat16).astype(jnp.float32)
    delta = own_edge_product - blind_product[:, :2].T
    start_part = jnp.sum((weight * start_state)[:, :, None] * full_powers, axis=1)
    conv_out = (
        conv_blind + start_part + long_taps * delta[0][:, None] + later_taps * delta[1][:, None]
    ).T
    short_query = jnp.concatenate([own_edge[:, 0], blind[2:, 0]], axis=0)
    gated = (short_query * conv_out).astype(jnp.bfloat16)
    tp_count = lax.axis_size("tp")
    pair_weight = out_weight.reshape(chan_count, tp_count // 2, 2, width_all // tp_count)
    even_part = jnp.einsum(
        "tc,cid->itd", gated, pair_weight[:, :, 0], preferred_element_type=jnp.float32
    )
    odd_part = jnp.einsum(
        "tc,cid->itd", gated, pair_weight[:, :, 1], preferred_element_type=jnp.float32
    )
    is_even = lax.axis_index("tp") % 2 == 0
    kept = jnp.where(is_even, even_part, odd_part)
    given = jnp.where(is_even, odd_part, even_part).astype(jnp.bfloat16)
    from_sibling = lax.ppermute(given, "tp", [(i, i ^ 1) for i in range(tp_count)])
    chip_sum = (kept + from_sibling.astype(jnp.float32)).astype(jnp.bfloat16)
    same_core = [[2 * i + c for i in range(tp_count // 2)] for c in range(2)]
    received = lax.all_to_all(
        chip_sum, "tp", split_axis=0, concat_axis=0, axis_index_groups=same_core
    )
    own_share = jnp.sum(received.astype(jnp.float32), axis=0)
    hyena_out = (resid_in.astype(jnp.float32) + own_share).astype(jnp.bfloat16)
    wide = gather_by_exchange(hyena_out, "tp", concat_axis=0).astype(jnp.float32)
    mean_square = jnp.sum(wide * wide, axis=(0, 2), keepdims=True) / width_all
    gain_blocks = norm_gain.reshape(tp_count, 1, chan_count)
    normed = (wide * lax.rsqrt(mean_square + eps_norm) * gain_blocks).astype(jnp.bfloat16)
    projected = jnp.einsum(
        "jtc,jcpd->tpd",
        normed,
        attn_weight.reshape(tp_count, chan_count, 3, chan_count),
        preferred_element_type=jnp.float32,
    )
    head_count = chan_count // HEAD_DIM
    first_pos = ctx_index * row_count
    positions = first_pos + jnp.arange(row_count, dtype=jnp.int32)
    queries = rotary_turn(
        projected[:, 0].reshape(row_count, head_count, HEAD_DIM), positions
    ).astype(jnp.bfloat16)
    keys_all = rotary_turn(
        projected[:, 1].reshape(row_count, head_count, HEAD_DIM), positions
    ).astype(jnp.bfloat16)
    values = projected[:, 2].astype(jnp.bfloat16)
    joined_kv = jnp.concatenate([keys_all.reshape(row_count, chan_count), values], axis=1)
    gathered_kv = gather_by_exchange(joined_kv, "ctx", concat_axis=0)
    gathered_kv = gathered_kv.reshape(ctx_count * row_count, 2 * chan_count)
    key_total = gathered_kv.shape[0]
    key_rows = gathered_kv[:, :chan_count].reshape(key_total, head_count, HEAD_DIM)
    value_rows = gathered_kv[:, chan_count:].reshape(key_total, head_count, HEAD_DIM)
    key_pos = jnp.arange(key_total, dtype=jnp.int32)
    scores = jnp.einsum(
        "shd,khd->hsk", queries, key_rows, preferred_element_type=jnp.float32
    ) * (1.0 / math.sqrt(HEAD_DIM))
    allowed = (positions[:, None] >= key_pos[None, :])[None]
    masked = jnp.where(allowed, scores, mask_fill)
    run_peak = jnp.max(masked, axis=2, keepdims=True)
    probs = jnp.where(allowed, jnp.exp(masked - run_peak), 0.0)
    denom = jnp.sum(probs, axis=2, keepdims=True)
    summed = jnp.einsum(
        "hsk,khd->hsd", probs.astype(jnp.bfloat16), value_rows, preferred_element_type=jnp.float32
    )
    heads_out = summed / denom
    context = heads_out.transpose(1, 0, 2).reshape(row_count, chan_count).astype(jnp.bfloat16)
    return (hyena_out, context)


def solution(mesh):
    in_specs = (
        P("ctx", "tp"),
        P("ctx", None, "tp"),
        P(None, None, "tp"),
        P("tp", None),
        P("tp", None),
        P("tp", None),
        P(),
        P(None, None, "tp"),
    )
    out_specs = (P("ctx", "tp"), P("ctx", "tp"))
    return jax.shard_map(
        per_device, mesh=mesh, in_specs=in_specs, out_specs=out_specs, check_vma=False
    )
```

```python
import math

import jax
import jax.numpy as jnp
from jax import lax
from jax.sharding import PartitionSpec as P

HEAD_DIM = 128


eps_norm = 1e-05
rope_base = 10000.0
mask_fill = -1e30
highest = lax.Precision.HIGHEST


def gather_by_exchange(block, axis, concat_axis=1):
    count = lax.axis_size(axis)
    copies = jnp.broadcast_to(block[None], (count,) + block.shape)
    return lax.all_to_all(copies, axis, split_axis=0, concat_axis=concat_axis, tiled=False)


def toeplitz_lower(filter_taps):
    chan_count, block_size = filter_taps.shape
    padded = jnp.concatenate(
        [jnp.zeros((chan_count, block_size - 1), jnp.float32), filter_taps], axis=1
    )
    flipped = padded[:, ::-1]
    tiled = jnp.tile(flipped, (1, block_size))
    offset = block_size - 1
    window = tiled[:, offset : offset + block_size * (2 * block_size - 2)]
    return window.reshape(chan_count, block_size, 2 * block_size - 2)[:, :, :block_size]


def modal_conv(signal, residues, rates, start_state, block_limit=128):
    chan_count, length = signal.shape
    block_size = math.gcd(length, block_limit)
    block_count = length // block_size
    weight = residues * jnp.sqrt(1.0 - jnp.exp(-2.0 * rates))
    lag_steps = jnp.arange(block_size, dtype=jnp.float32)
    powers = jnp.exp(-rates[:, :, None] * lag_steps)
    filter_taps = jnp.sum(weight[:, :, None] * powers, axis=1)
    toeplitz = toeplitz_lower(filter_taps)
    blocks = signal.reshape(chan_count, block_count, block_size)
    inner_part = jnp.einsum("cij,cnj->cni", toeplitz, blocks, precision=highest)
    tail_powers = jnp.exp(-rates[:, :, None] * (block_size - lag_steps))
    end_states = jnp.einsum("cnj,cmj->cnm", blocks, tail_powers, precision=highest)
    block_steps = jnp.arange(block_count, dtype=jnp.float32)
    gap_count = block_steps[:, None] - 1.0 - block_steps[None, :]
    live_mask = gap_count >= 0.0
    carry_mat = jnp.where(
        live_mask, jnp.exp(-rates[:, :, None, None] * block_size * jnp.maximum(gap_count, 0.0)), 0.0
    )
    states = jnp.einsum("cmnk,ckm->cnm", carry_mat, end_states, precision=highest)
    states = (
        states
        + jnp.exp(-rates[:, None, :] * block_size * block_steps[None, :, None])
        * start_state[:, None, :]
    )
    cross_part = jnp.einsum("cnm,cmi->cni", states * weight[:, None, :], powers, precision=highest)
    return (inner_part + cross_part).reshape(chan_count, length)


def short_conv(joined, short_filter):
    row_count = joined.shape[0] - 2
    return (
        short_filter[0] * joined[2:]
        + short_filter[1] * joined[1 : row_count + 1]
        + short_filter[2] * joined[:row_count]
    )


def rotary_turn(vectors, positions):
    half_dim = vectors.shape[-1] // 2
    frequency = rope_base ** (-jnp.arange(half_dim, dtype=jnp.float32) * 2.0 / vectors.shape[-1])
    angles = positions.astype(jnp.float32)[:, None] * frequency[None, :]
    cosine = jnp.cos(angles)[:, None, :]
    sine_part = jnp.sin(angles)[:, None, :]
    first_half = vectors[..., :half_dim]
    second = vectors[..., half_dim:]
    return jnp.concatenate(
        [first_half * cosine - second * sine_part, second * cosine + first_half * sine_part],
        axis=-1,
    )


def per_device(resid_in, feats, short_filter, residues, rates, out_weight, norm_gain, attn_weight):
    row_count, chan_count = resid_in.shape
    width_all = out_weight.shape[1]
    feats_wide = feats.astype(jnp.float32)
    ctx_count = lax.axis_size("ctx")
    ctx_index = lax.axis_index("ctx")
    lag_steps = jnp.arange(row_count, dtype=jnp.float32)
    tail_powers = jnp.exp(-rates[:, :, None] * (row_count - lag_steps))
    no_prior = jnp.zeros((2,) + feats_wide.shape[1:], jnp.float32)
    blind = short_conv(jnp.concatenate([no_prior, feats_wide], axis=0), short_filter)
    blind_product = (blind[:, 1] * blind[:, 2]).astype(jnp.bfloat16).T.astype(jnp.float32)
    late_state = jnp.einsum(
        "ct,cmt->cm", blind_product[:, 2:], tail_powers[:, :, 2:], precision=highest
    )
    mode_count = late_state.shape[1]
    head_rows = feats_wide[:2, 1:, :].reshape(4, chan_count)
    tail_rows = feats_wide[-2:].reshape(6, chan_count)
    payload = jnp.concatenate([late_state.T, head_rows, tail_rows], axis=0)
    received = gather_by_exchange(payload, "ctx", concat_axis=0)
    late_all = received[:, :mode_count]
    head_all = received[:, mode_count : mode_count + 4].reshape(ctx_count, 2, 2, chan_count)
    tail_all = received[:, mode_count + 4 :].reshape(ctx_count, 2, 3, chan_count)
    prev_tail = jnp.concatenate([jnp.zeros_like(tail_all[:1]), tail_all[:-1]], axis=0)
    edge_joined = jnp.concatenate([prev_tail[:, :, 1:], head_all], axis=1)
    taps = short_filter[:, 1:, :]
    edge_short = taps[0] * edge_joined[:, 2:] + taps[1] * edge_joined[:, 1:3] + taps[2] * edge_joined[:, :2]
    edge_product = (edge_short[:, :, 0] * edge_short[:, :, 1]).astype(jnp.bfloat16).astype(jnp.float32)
    first_powers = tail_powers[:, :, 0].T
    second_powers = tail_powers[:, :, 1].T
    gathered_states = (
        late_all
        + edge_product[:, 0:1, :] * first_powers[None]
        + edge_product[:, 1:2, :] * second_powers[None]
    )
    shard_steps = jnp.arange(ctx_count, dtype=jnp.float32)
    gap_count = ctx_index.astype(jnp.float32) - 1.0 - shard_steps
    decay = jnp.where(
        (gap_count >= 0.0)[:, None, None],
        jnp.exp(-rates.T[None] * row_count * jnp.maximum(gap_count, 0.0)[:, None, None]),
        0.0,
    )
    start_state = jnp.sum(decay * gathered_states, axis=0).T
    conv_blind = modal_conv(
        blind_product, residues, rates, jnp.zeros_like(rates), block_limit=16
    )
    weight = residues * jnp.sqrt(1.0 - jnp.exp(-2.0 * rates))
    full_powers = jnp.exp(-rates[:, :, None] * lag_steps)
    long_taps = jnp.sum(weight[:, :, None] * full_powers, axis=1)
    later_taps = jnp.concatenate([jnp.zeros_like(long_taps[:, :1]), long_taps[:, :-1]], axis=1)
    own_prior = lax.dynamic_index_in_dim(prev_tail, ctx_index, 0, keepdims=False)
    own_edge = short_conv(jnp.concatenate([own_prior, feats_wide[:2]], axis=0), short_filter)
    own_edge_product = (own_edge[:, 1] * own_edge[:, 2]).astype(jnp.bfloat16).astype(jnp.float32)
    delta = own_edge_product - blind_product[:, :2].T
    start_part = jnp.sum((weight * start_state)[:, :, None] * full_powers, axis=1)
    conv_out = (
        conv_blind + start_part + long_taps * delta[0][:, None] + later_taps * delta[1][:, None]
    ).T
    short_query = jnp.concatenate([own_edge[:, 0], blind[2:, 0]], axis=0)
    gated = (short_query * conv_out).astype(jnp.bfloat16)
    tp_count = lax.axis_size("tp")
    pair_weight = out_weight.reshape(chan_count, tp_count // 2, 2, width_all // tp_count)
    even_part = jnp.einsum(
        "tc,cid->itd", gated, pair_weight[:, :, 0], preferred_element_type=jnp.float32
    )
    odd_part = jnp.einsum(
        "tc,cid->itd", gated, pair_weight[:, :, 1], preferred_element_type=jnp.float32
    )
    is_even = lax.axis_index("tp") % 2 == 0
    kept = jnp.where(is_even, even_part, odd_part)
    given = jnp.where(is_even, odd_part, even_part).astype(jnp.bfloat16)
    from_sibling = lax.ppermute(given, "tp", [(i, i ^ 1) for i in range(tp_count)])
    chip_sum = (kept + from_sibling.astype(jnp.float32)).astype(jnp.bfloat16)
    same_core = [[2 * i + c for i in range(tp_count // 2)] for c in range(2)]
    received = lax.all_to_all(
        chip_sum, "tp", split_axis=0, concat_axis=0, axis_index_groups=same_core
    )
    own_share = jnp.sum(received.astype(jnp.float32), axis=0)
    hyena_out = (resid_in.astype(jnp.float32) + own_share).astype(jnp.bfloat16)
    full_rows = gather_by_exchange(hyena_out, "tp").reshape(row_count, width_all)
    wide = full_rows.astype(jnp.float32)
    mean_square = jnp.mean(wide * wide, axis=1, keepdims=True)
    normed = (wide * lax.rsqrt(mean_square + eps_norm) * norm_gain).astype(jnp.bfloat16)
    projected = jnp.dot(
        normed, attn_weight.reshape(width_all, 3 * chan_count), preferred_element_type=jnp.float32
    ).reshape(row_count, 3, chan_count)
    head_count = chan_count // HEAD_DIM
    first_pos = ctx_index * row_count
    positions = first_pos + jnp.arange(row_count, dtype=jnp.int32)
    queries = rotary_turn(
        projected[:, 0].reshape(row_count, head_count, HEAD_DIM), positions
    ).astype(jnp.bfloat16)
    keys_all = rotary_turn(
        projected[:, 1].reshape(row_count, head_count, HEAD_DIM), positions
    ).astype(jnp.bfloat16)
    values = projected[:, 2].astype(jnp.bfloat16)
    joined_kv = jnp.concatenate([keys_all.reshape(row_count, chan_count), values], axis=1)
    gathered_kv = gather_by_exchange(joined_kv, "ctx", concat_axis=0)
    gathered_kv = gathered_kv.reshape(ctx_count * row_count, 2 * chan_count)
    key_total = gathered_kv.shape[0]
    key_rows = gathered_kv[:, :chan_count].reshape(key_total, head_count, HEAD_DIM)
    value_rows = gathered_kv[:, chan_count:].reshape(key_total, head_count, HEAD_DIM)
    key_pos = jnp.arange(key_total, dtype=jnp.int32)
    scores = jnp.einsum(
        "shd,khd->hsk", queries, key_rows, preferred_element_type=jnp.float32
    ) * (1.0 / math.sqrt(HEAD_DIM))
    allowed = (positions[:, None] >= key_pos[None, :])[None]
    masked = jnp.where(allowed, scores, mask_fill)
    run_peak = jnp.max(masked, axis=2, keepdims=True)
    probs = jnp.where(allowed, jnp.exp(masked - run_peak), 0.0)
    denom = jnp.sum(probs, axis=2, keepdims=True)
    summed = jnp.einsum(
        "hsk,khd->hsd", probs.astype(jnp.bfloat16), value_rows, preferred_element_type=jnp.float32
    )
    heads_out = summed / denom
    context = heads_out.transpose(1, 0, 2).reshape(row_count, chan_count).astype(jnp.bfloat16)
    return (hyena_out, context)


def solution(mesh):
    in_specs = (
        P("ctx", "tp"),
        P("ctx", None, "tp"),
        P(None, None, "tp"),
        P("tp", None),
        P("tp", None),
        P("tp", None),
        P(),
        P(None, None, "tp"),
    )
    out_specs = (P("ctx", "tp"), P("ctx", "tp"))
    return jax.shard_map(
        per_device, mesh=mesh, in_specs=in_specs, out_specs=out_specs, check_vma=False
    )
```

```python
import math

import jax
import jax.numpy as jnp
from jax import lax
from jax.sharding import PartitionSpec as P

HEAD_DIM = 128


eps_norm = 1e-05
rope_base = 10000.0
mask_fill = -1e30
highest = lax.Precision.HIGHEST


def gather_by_exchange(block, axis, concat_axis=1):
    count = lax.axis_size(axis)
    copies = jnp.broadcast_to(block[None], (count,) + block.shape)
    return lax.all_to_all(copies, axis, split_axis=0, concat_axis=concat_axis, tiled=False)


def toeplitz_lower(filter_taps):
    chan_count, block_size = filter_taps.shape
    padded = jnp.concatenate(
        [jnp.zeros((chan_count, block_size - 1), jnp.float32), filter_taps], axis=1
    )
    flipped = padded[:, ::-1]
    tiled = jnp.tile(flipped, (1, block_size))
    offset = block_size - 1
    window = tiled[:, offset : offset + block_size * (2 * block_size - 2)]
    return window.reshape(chan_count, block_size, 2 * block_size - 2)[:, :, :block_size]


def modal_conv(signal, residues, rates, start_state, block_limit=128):
    chan_count, length = signal.shape
    block_size = math.gcd(length, block_limit)
    block_count = length // block_size
    weight = residues * jnp.sqrt(1.0 - jnp.exp(-2.0 * rates))
    lag_steps = jnp.arange(block_size, dtype=jnp.float32)
    powers = jnp.exp(-rates[:, :, None] * lag_steps)
    filter_taps = jnp.sum(weight[:, :, None] * powers, axis=1)
    toeplitz = toeplitz_lower(filter_taps)
    blocks = signal.reshape(chan_count, block_count, block_size)
    inner_part = jnp.einsum("cij,cnj->cni", toeplitz, blocks, precision=highest)
    tail_powers = jnp.exp(-rates[:, :, None] * (block_size - lag_steps))
    end_states = jnp.einsum("cnj,cmj->cnm", blocks, tail_powers, precision=highest)
    block_steps = jnp.arange(block_count, dtype=jnp.float32)
    gap_count = block_steps[:, None] - 1.0 - block_steps[None, :]
    live_mask = gap_count >= 0.0
    carry_mat = jnp.where(
        live_mask, jnp.exp(-rates[:, :, None, None] * block_size * jnp.maximum(gap_count, 0.0)), 0.0
    )
    states = jnp.einsum("cmnk,ckm->cnm", carry_mat, end_states, precision=highest)
    states = (
        states
        + jnp.exp(-rates[:, None, :] * block_size * block_steps[None, :, None])
        * start_state[:, None, :]
    )
    cross_part = jnp.einsum("cnm,cmi->cni", states * weight[:, None, :], powers, precision=highest)
    return (inner_part + cross_part).reshape(chan_count, length)


def short_conv(joined, short_filter):
    row_count = joined.shape[0] - 2
    return (
        short_filter[0] * joined[2:]
        + short_filter[1] * joined[1 : row_count + 1]
        + short_filter[2] * joined[:row_count]
    )


def rotary_turn(vectors, positions):
    half_dim = vectors.shape[-1] // 2
    frequency = rope_base ** (-jnp.arange(half_dim, dtype=jnp.float32) * 2.0 / vectors.shape[-1])
    angles = positions.astype(jnp.float32)[:, None] * frequency[None, :]
    cosine = jnp.cos(angles)[:, None, :]
    sine_part = jnp.sin(angles)[:, None, :]
    first_half = vectors[..., :half_dim]
    second = vectors[..., half_dim:]
    return jnp.concatenate(
        [first_half * cosine - second * sine_part, second * cosine + first_half * sine_part],
        axis=-1,
    )


def per_device(resid_in, feats, short_filter, residues, rates, out_weight, norm_gain, attn_weight):
    row_count, chan_count = resid_in.shape
    width_all = out_weight.shape[1]
    feats_wide = feats.astype(jnp.float32)
    ctx_count = lax.axis_size("ctx")
    ctx_index = lax.axis_index("ctx")
    lag_steps = jnp.arange(row_count, dtype=jnp.float32)
    tail_powers = jnp.exp(-rates[:, :, None] * (row_count - lag_steps))
    no_prior = jnp.zeros((2,) + feats_wide.shape[1:], jnp.float32)
    blind = short_conv(jnp.concatenate([no_prior, feats_wide], axis=0), short_filter)
    blind_product = (blind[:, 1] * blind[:, 2]).astype(jnp.bfloat16).T.astype(jnp.float32)
    late_state = jnp.einsum(
        "ct,cmt->cm", blind_product[:, 2:], tail_powers[:, :, 2:], precision=highest
    )
    mode_count = late_state.shape[1]
    head_rows = feats_wide[:2, 1:, :].reshape(4, chan_count)
    tail_rows = feats_wide[-2:].reshape(6, chan_count)
    payload = jnp.concatenate([late_state.T, head_rows, tail_rows], axis=0)
    received = gather_by_exchange(payload, "ctx", concat_axis=0)
    conv_blind = modal_conv(
        blind_product, residues, rates, jnp.zeros_like(rates), block_limit=16
    )
    weight = residues * jnp.sqrt(1.0 - jnp.exp(-2.0 * rates))
    full_powers = jnp.exp(-rates[:, :, None] * lag_steps)
    long_taps = jnp.sum(weight[:, :, None] * full_powers, axis=1)
    later_taps = jnp.concatenate([jnp.zeros_like(long_taps[:, :1]), long_taps[:, :-1]], axis=1)
    received, conv_blind, long_taps, later_taps, full_powers = lax.optimization_barrier(
        (received, conv_blind, long_taps, later_taps, full_powers)
    )
    late_all = received[:, :mode_count]
    head_all = received[:, mode_count : mode_count + 4].reshape(ctx_count, 2, 2, chan_count)
    tail_all = received[:, mode_count + 4 :].reshape(ctx_count, 2, 3, chan_count)
    prev_tail = jnp.concatenate([jnp.zeros_like(tail_all[:1]), tail_all[:-1]], axis=0)
    edge_joined = jnp.concatenate([prev_tail[:, :, 1:], head_all], axis=1)
    taps = short_filter[:, 1:, :]
    edge_short = taps[0] * edge_joined[:, 2:] + taps[1] * edge_joined[:, 1:3] + taps[2] * edge_joined[:, :2]
    edge_product = (edge_short[:, :, 0] * edge_short[:, :, 1]).astype(jnp.bfloat16).astype(jnp.float32)
    first_powers = tail_powers[:, :, 0].T
    second_powers = tail_powers[:, :, 1].T
    gathered_states = (
        late_all
        + edge_product[:, 0:1, :] * first_powers[None]
        + edge_product[:, 1:2, :] * second_powers[None]
    )
    shard_steps = jnp.arange(ctx_count, dtype=jnp.float32)
    gap_count = ctx_index.astype(jnp.float32) - 1.0 - shard_steps
    decay = jnp.where(
        (gap_count >= 0.0)[:, None, None],
        jnp.exp(-rates.T[None] * row_count * jnp.maximum(gap_count, 0.0)[:, None, None]),
        0.0,
    )
    start_state = jnp.sum(decay * gathered_states, axis=0).T
    own_prior = lax.dynamic_index_in_dim(prev_tail, ctx_index, 0, keepdims=False)
    own_edge = short_conv(jnp.concatenate([own_prior, feats_wide[:2]], axis=0), short_filter)
    own_edge_product = (own_edge[:, 1] * own_edge[:, 2]).astype(jnp.bfloat16).astype(jnp.float32)
    delta = own_edge_product - blind_product[:, :2].T
    start_part = jnp.sum((weight * start_state)[:, :, None] * full_powers, axis=1)
    conv_out = (
        conv_blind + start_part + long_taps * delta[0][:, None] + later_taps * delta[1][:, None]
    ).T
    short_query = jnp.concatenate([own_edge[:, 0], blind[2:, 0]], axis=0)
    gated = (short_query * conv_out).astype(jnp.bfloat16)
    tp_count = lax.axis_size("tp")
    pair_weight = out_weight.reshape(chan_count, tp_count // 2, 2, width_all // tp_count)
    even_part = jnp.einsum(
        "tc,cid->itd", gated, pair_weight[:, :, 0], preferred_element_type=jnp.float32
    )
    odd_part = jnp.einsum(
        "tc,cid->itd", gated, pair_weight[:, :, 1], preferred_element_type=jnp.float32
    )
    is_even = lax.axis_index("tp") % 2 == 0
    kept = jnp.where(is_even, even_part, odd_part)
    given = jnp.where(is_even, odd_part, even_part).astype(jnp.bfloat16)
    from_sibling = lax.ppermute(given, "tp", [(i, i ^ 1) for i in range(tp_count)])
    chip_sum = (kept + from_sibling.astype(jnp.float32)).astype(jnp.bfloat16)
    same_core = [[2 * i + c for i in range(tp_count // 2)] for c in range(2)]
    received = lax.all_to_all(
        chip_sum, "tp", split_axis=0, concat_axis=0, axis_index_groups=same_core
    )
    own_share = jnp.sum(received.astype(jnp.float32), axis=0)
    hyena_out = (resid_in.astype(jnp.float32) + own_share).astype(jnp.bfloat16)
    full_rows = gather_by_exchange(hyena_out, "tp").reshape(row_count, width_all)
    wide = full_rows.astype(jnp.float32)
    mean_square = jnp.mean(wide * wide, axis=1, keepdims=True)
    normed = (wide * lax.rsqrt(mean_square + eps_norm) * norm_gain).astype(jnp.bfloat16)
    projected = jnp.dot(
        normed, attn_weight.reshape(width_all, 3 * chan_count), preferred_element_type=jnp.float32
    ).reshape(row_count, 3, chan_count)
    head_count = chan_count // HEAD_DIM
    first_pos = ctx_index * row_count
    positions = first_pos + jnp.arange(row_count, dtype=jnp.int32)
    queries = rotary_turn(
        projected[:, 0].reshape(row_count, head_count, HEAD_DIM), positions
    ).astype(jnp.bfloat16)
    keys_all = rotary_turn(
        projected[:, 1].reshape(row_count, head_count, HEAD_DIM), positions
    ).astype(jnp.bfloat16)
    values = projected[:, 2].astype(jnp.bfloat16)
    joined_kv = jnp.concatenate([keys_all.reshape(row_count, chan_count), values], axis=1)
    gathered_kv = gather_by_exchange(joined_kv, "ctx", concat_axis=0)
    gathered_kv = gathered_kv.reshape(ctx_count * row_count, 2 * chan_count)
    key_total = gathered_kv.shape[0]
    key_rows = gathered_kv[:, :chan_count].reshape(key_total, head_count, HEAD_DIM)
    value_rows = gathered_kv[:, chan_count:].reshape(key_total, head_count, HEAD_DIM)
    key_pos = jnp.arange(key_total, dtype=jnp.int32)
    scores = jnp.einsum(
        "shd,khd->hsk", queries, key_rows, preferred_element_type=jnp.float32
    ) * (1.0 / math.sqrt(HEAD_DIM))
    allowed = (positions[:, None] >= key_pos[None, :])[None]
    masked = jnp.where(allowed, scores, mask_fill)
    run_peak = jnp.max(masked, axis=2, keepdims=True)
    probs = jnp.where(allowed, jnp.exp(masked - run_peak), 0.0)
    denom = jnp.sum(probs, axis=2, keepdims=True)
    summed = jnp.einsum(
        "hsk,khd->hsd", probs.astype(jnp.bfloat16), value_rows, preferred_element_type=jnp.float32
    )
    heads_out = summed / denom
    context = heads_out.transpose(1, 0, 2).reshape(row_count, chan_count).astype(jnp.bfloat16)
    return (hyena_out, context)


def solution(mesh):
    in_specs = (
        P("ctx", "tp"),
        P("ctx", None, "tp"),
        P(None, None, "tp"),
        P("tp", None),
        P("tp", None),
        P("tp", None),
        P(),
        P(None, None, "tp"),
    )
    out_specs = (P("ctx", "tp"), P("ctx", "tp"))
    return jax.shard_map(
        per_device, mesh=mesh, in_specs=in_specs, out_specs=out_specs, check_vma=False
    )
```

```python
import math

import jax
import jax.numpy as jnp
from jax import lax
from jax.sharding import PartitionSpec as P

HEAD_DIM = 128


eps_norm = 1e-05
rope_base = 10000.0
mask_fill = -1e30
highest = lax.Precision.HIGHEST


def gather_by_exchange(block, axis, concat_axis=1):
    count = lax.axis_size(axis)
    copies = jnp.broadcast_to(block[None], (count,) + block.shape)
    return lax.all_to_all(copies, axis, split_axis=0, concat_axis=concat_axis, tiled=False)


def toeplitz_lower(filter_taps):
    chan_count, block_size = filter_taps.shape
    padded = jnp.concatenate(
        [jnp.zeros((chan_count, block_size - 1), jnp.float32), filter_taps], axis=1
    )
    flipped = padded[:, ::-1]
    tiled = jnp.tile(flipped, (1, block_size))
    offset = block_size - 1
    window = tiled[:, offset : offset + block_size * (2 * block_size - 2)]
    return window.reshape(chan_count, block_size, 2 * block_size - 2)[:, :, :block_size]


def modal_conv(signal, residues, rates, start_state, block_limit=128):
    chan_count, length = signal.shape
    block_size = math.gcd(length, block_limit)
    block_count = length // block_size
    weight = residues * jnp.sqrt(1.0 - jnp.exp(-2.0 * rates))
    lag_steps = jnp.arange(block_size, dtype=jnp.float32)
    powers = jnp.exp(-rates[:, :, None] * lag_steps)
    filter_taps = jnp.sum(weight[:, :, None] * powers, axis=1)
    toeplitz = toeplitz_lower(filter_taps)
    blocks = signal.reshape(chan_count, block_count, block_size)
    inner_part = jnp.einsum("cij,cnj->cni", toeplitz, blocks, precision=highest)
    tail_powers = jnp.exp(-rates[:, :, None] * (block_size - lag_steps))
    end_states = jnp.einsum("cnj,cmj->cnm", blocks, tail_powers, precision=highest)
    block_steps = jnp.arange(block_count, dtype=jnp.float32)
    gap_count = block_steps[:, None] - 1.0 - block_steps[None, :]
    live_mask = gap_count >= 0.0
    carry_mat = jnp.where(
        live_mask, jnp.exp(-rates[:, :, None, None] * block_size * jnp.maximum(gap_count, 0.0)), 0.0
    )
    states = jnp.einsum("cmnk,ckm->cnm", carry_mat, end_states, precision=highest)
    states = (
        states
        + jnp.exp(-rates[:, None, :] * block_size * block_steps[None, :, None])
        * start_state[:, None, :]
    )
    cross_part = jnp.einsum("cnm,cmi->cni", states * weight[:, None, :], powers, precision=highest)
    return (inner_part + cross_part).reshape(chan_count, length)


def short_conv(joined, short_filter):
    row_count = joined.shape[0] - 2
    return (
        short_filter[0] * joined[2:]
        + short_filter[1] * joined[1 : row_count + 1]
        + short_filter[2] * joined[:row_count]
    )


def rotary_turn(vectors, positions):
    half_dim = vectors.shape[-1] // 2
    frequency = rope_base ** (-jnp.arange(half_dim, dtype=jnp.float32) * 2.0 / vectors.shape[-1])
    angles = positions.astype(jnp.float32)[:, None] * frequency[None, :]
    cosine = jnp.cos(angles)[:, None, :]
    sine_part = jnp.sin(angles)[:, None, :]
    first_half = vectors[..., :half_dim]
    second = vectors[..., half_dim:]
    return jnp.concatenate(
        [first_half * cosine - second * sine_part, second * cosine + first_half * sine_part],
        axis=-1,
    )


def per_device(resid_in, feats, short_filter, residues, rates, out_weight, norm_gain, attn_weight):
    row_count, chan_count = resid_in.shape
    width_all = out_weight.shape[1]
    feats_wide = feats.astype(jnp.float32)
    ctx_count = lax.axis_size("ctx")
    ctx_index = lax.axis_index("ctx")
    lag_steps = jnp.arange(row_count, dtype=jnp.float32)
    tail_powers = jnp.exp(-rates[:, :, None] * (row_count - lag_steps))
    no_prior = jnp.zeros((2,) + feats_wide.shape[1:], jnp.float32)
    blind = short_conv(jnp.concatenate([no_prior, feats_wide], axis=0), short_filter)
    blind_product = (blind[:, 1] * blind[:, 2]).astype(jnp.bfloat16).T.astype(jnp.float32)
    late_state = jnp.einsum(
        "ct,cmt->cm", blind_product[:, 2:], tail_powers[:, :, 2:], precision=highest
    )
    mode_count = late_state.shape[1]
    head_rows = feats_wide[:2, 1:, :].reshape(4, chan_count)
    tail_rows = feats_wide[-2:].reshape(6, chan_count)
    payload = jnp.concatenate([late_state.T, head_rows, tail_rows], axis=0)
    received = gather_by_exchange(payload, "ctx", concat_axis=0)
    conv_blind = modal_conv(
        blind_product, residues, rates, jnp.zeros_like(rates), block_limit=16
    )
    weight = residues * jnp.sqrt(1.0 - jnp.exp(-2.0 * rates))
    full_powers = jnp.exp(-rates[:, :, None] * lag_steps)
    long_taps = jnp.sum(weight[:, :, None] * full_powers, axis=1)
    later_taps = jnp.concatenate([jnp.zeros_like(long_taps[:, :1]), long_taps[:, :-1]], axis=1)
    received, conv_blind, long_taps, later_taps, full_powers = lax.optimization_barrier(
        (received, conv_blind, long_taps, later_taps, full_powers)
    )
    late_all = received[:, :mode_count]
    head_all = received[:, mode_count : mode_count + 4].reshape(ctx_count, 2, 2, chan_count)
    tail_all = received[:, mode_count + 4 :].reshape(ctx_count, 2, 3, chan_count)
    prev_tail = jnp.concatenate([jnp.zeros_like(tail_all[:1]), tail_all[:-1]], axis=0)
    edge_joined = jnp.concatenate([prev_tail[:, :, 1:], head_all], axis=1)
    taps = short_filter[:, 1:, :]
    edge_short = taps[0] * edge_joined[:, 2:] + taps[1] * edge_joined[:, 1:3] + taps[2] * edge_joined[:, :2]
    edge_product = (edge_short[:, :, 0] * edge_short[:, :, 1]).astype(jnp.bfloat16).astype(jnp.float32)
    first_powers = tail_powers[:, :, 0].T
    second_powers = tail_powers[:, :, 1].T
    gathered_states = (
        late_all
        + edge_product[:, 0:1, :] * first_powers[None]
        + edge_product[:, 1:2, :] * second_powers[None]
    )
    shard_steps = jnp.arange(ctx_count, dtype=jnp.float32)
    gap_count = ctx_index.astype(jnp.float32) - 1.0 - shard_steps
    decay = jnp.where(
        (gap_count >= 0.0)[:, None, None],
        jnp.exp(-rates.T[None] * row_count * jnp.maximum(gap_count, 0.0)[:, None, None]),
        0.0,
    )
    start_state = jnp.sum(decay * gathered_states, axis=0).T
    own_prior = lax.dynamic_index_in_dim(prev_tail, ctx_index, 0, keepdims=False)
    own_edge = short_conv(jnp.concatenate([own_prior, feats_wide[:2]], axis=0), short_filter)
    own_edge_product = (own_edge[:, 1] * own_edge[:, 2]).astype(jnp.bfloat16).astype(jnp.float32)
    delta = own_edge_product - blind_product[:, :2].T
    start_part = jnp.sum((weight * start_state)[:, :, None] * full_powers, axis=1)
    conv_out = (
        conv_blind + start_part + long_taps * delta[0][:, None] + later_taps * delta[1][:, None]
    ).T
    short_query = jnp.concatenate([own_edge[:, 0], blind[2:, 0]], axis=0)
    gated = (short_query * conv_out).astype(jnp.bfloat16)
    tp_count = lax.axis_size("tp")
    pair_weight = out_weight.reshape(chan_count, tp_count // 2, 2, width_all // tp_count)
    even_part = jnp.einsum(
        "tc,cid->itd", gated, pair_weight[:, :, 0], preferred_element_type=jnp.float32
    )
    odd_part = jnp.einsum(
        "tc,cid->itd", gated, pair_weight[:, :, 1], preferred_element_type=jnp.float32
    )
    is_even = lax.axis_index("tp") % 2 == 0
    kept = jnp.where(is_even, even_part, odd_part)
    given = jnp.where(is_even, odd_part, even_part).astype(jnp.bfloat16)
    from_sibling = lax.ppermute(given, "tp", [(i, i ^ 1) for i in range(tp_count)])
    chip_sum = (kept + from_sibling.astype(jnp.float32)).astype(jnp.bfloat16)
    same_core = [[2 * i + c for i in range(tp_count // 2)] for c in range(2)]
    received = lax.all_to_all(
        chip_sum, "tp", split_axis=0, concat_axis=0, axis_index_groups=same_core
    )
    own_share = jnp.sum(received.astype(jnp.float32), axis=0)
    hyena_out = (resid_in.astype(jnp.float32) + own_share).astype(jnp.bfloat16)
    full_rows = gather_by_exchange(hyena_out, "tp").reshape(row_count, width_all)
    wide = full_rows.astype(jnp.float32)
    mean_square = jnp.mean(wide * wide, axis=1, keepdims=True)
    scaled = (wide * norm_gain).astype(jnp.bfloat16)
    projected = (
        jnp.dot(
            scaled, attn_weight.reshape(width_all, 3 * chan_count), preferred_element_type=jnp.float32
        )
        * lax.rsqrt(mean_square + eps_norm)
    ).reshape(row_count, 3, chan_count)
    head_count = chan_count // HEAD_DIM
    first_pos = ctx_index * row_count
    positions = first_pos + jnp.arange(row_count, dtype=jnp.int32)
    queries = rotary_turn(
        projected[:, 0].reshape(row_count, head_count, HEAD_DIM), positions
    ).astype(jnp.bfloat16)
    keys_all = rotary_turn(
        projected[:, 1].reshape(row_count, head_count, HEAD_DIM), positions
    ).astype(jnp.bfloat16)
    values = projected[:, 2].astype(jnp.bfloat16)
    joined_kv = jnp.concatenate([keys_all.reshape(row_count, chan_count), values], axis=1)
    gathered_kv = gather_by_exchange(joined_kv, "ctx", concat_axis=0)
    gathered_kv = gathered_kv.reshape(ctx_count * row_count, 2 * chan_count)
    key_total = gathered_kv.shape[0]
    key_rows = gathered_kv[:, :chan_count].reshape(key_total, head_count, HEAD_DIM)
    value_rows = gathered_kv[:, chan_count:].reshape(key_total, head_count, HEAD_DIM)
    key_pos = jnp.arange(key_total, dtype=jnp.int32)
    scores = jnp.einsum(
        "shd,khd->hsk", queries, key_rows, preferred_element_type=jnp.float32
    ) * (1.0 / math.sqrt(HEAD_DIM))
    allowed = (positions[:, None] >= key_pos[None, :])[None]
    masked = jnp.where(allowed, scores, mask_fill)
    run_peak = jnp.max(masked, axis=2, keepdims=True)
    probs = jnp.where(allowed, jnp.exp(masked - run_peak), 0.0)
    denom = jnp.sum(probs, axis=2, keepdims=True)
    summed = jnp.einsum(
        "hsk,khd->hsd", probs.astype(jnp.bfloat16), value_rows, preferred_element_type=jnp.float32
    )
    heads_out = summed / denom
    context = heads_out.transpose(1, 0, 2).reshape(row_count, chan_count).astype(jnp.bfloat16)
    return (hyena_out, context)


def solution(mesh):
    in_specs = (
        P("ctx", "tp"),
        P("ctx", None, "tp"),
        P(None, None, "tp"),
        P("tp", None),
        P("tp", None),
        P("tp", None),
        P(),
        P(None, None, "tp"),
    )
    out_specs = (P("ctx", "tp"), P("ctx", "tp"))
    return jax.shard_map(
        per_device, mesh=mesh, in_specs=in_specs, out_specs=out_specs, check_vma=False
    )
```

```python
import math

import jax
import jax.numpy as jnp
from jax import lax
from jax.sharding import PartitionSpec as P

HEAD_DIM = 128


eps_norm = 1e-05
rope_base = 10000.0
mask_fill = -1e30
highest = lax.Precision.HIGHEST


def gather_by_exchange(block, axis, concat_axis=1):
    count = lax.axis_size(axis)
    copies = jnp.broadcast_to(block[None], (count,) + block.shape)
    return lax.all_to_all(copies, axis, split_axis=0, concat_axis=concat_axis, tiled=False)


def toeplitz_lower(filter_taps):
    chan_count, block_size = filter_taps.shape
    padded = jnp.concatenate(
        [jnp.zeros((chan_count, block_size - 1), jnp.float32), filter_taps], axis=1
    )
    flipped = padded[:, ::-1]
    tiled = jnp.tile(flipped, (1, block_size))
    offset = block_size - 1
    window = tiled[:, offset : offset + block_size * (2 * block_size - 2)]
    return window.reshape(chan_count, block_size, 2 * block_size - 2)[:, :, :block_size]


def modal_conv(signal, weight, rates, full_powers, block_size):
    chan_count, length = signal.shape
    block_count = length // block_size
    powers = full_powers[:, :, :block_size]
    filter_taps = jnp.sum(weight[:, :, None] * powers, axis=1)
    toeplitz = toeplitz_lower(filter_taps)
    blocks = signal.reshape(chan_count, block_count, block_size)
    inner_part = jnp.einsum("cij,cnj->cni", toeplitz, blocks, precision=highest)
    tail_powers = full_powers[:, :, block_size:0:-1]
    end_states = jnp.einsum("cnj,cmj->cnm", blocks, tail_powers, precision=highest)
    block_steps = jnp.arange(block_count, dtype=jnp.float32)
    gap_count = block_steps[:, None] - 1.0 - block_steps[None, :]
    live_mask = gap_count >= 0.0
    carry_mat = jnp.where(
        live_mask,
        jnp.exp(-rates[:, :, None, None] * block_size * jnp.maximum(gap_count, 0.0)),
        0.0,
    )
    states = jnp.einsum("cmnk,ckm->cnm", carry_mat, end_states, precision=highest)
    cross_part = jnp.einsum("cnm,cmi->cni", states * weight[:, None, :], powers, precision=highest)
    return (inner_part + cross_part).reshape(chan_count, length)


def short_conv(joined, short_filter):
    row_count = joined.shape[0] - 2
    return (
        short_filter[0] * joined[2:]
        + short_filter[1] * joined[1 : row_count + 1]
        + short_filter[2] * joined[:row_count]
    )


def rotary_turn(vectors, positions):
    half_dim = vectors.shape[-1] // 2
    frequency = rope_base ** (-jnp.arange(half_dim, dtype=jnp.float32) * 2.0 / vectors.shape[-1])
    angles = positions.astype(jnp.float32)[:, None] * frequency[None, :]
    cosine = jnp.cos(angles)[:, None, :]
    sine_part = jnp.sin(angles)[:, None, :]
    first_half = vectors[..., :half_dim]
    second = vectors[..., half_dim:]
    return jnp.concatenate(
        [first_half * cosine - second * sine_part, second * cosine + first_half * sine_part],
        axis=-1,
    )


def per_device(resid_in, feats, short_filter, residues, rates, out_weight, norm_gain, attn_weight):
    row_count, chan_count = resid_in.shape
    width_all = out_weight.shape[1]
    feats_wide = feats.astype(jnp.float32)
    ctx_count = lax.axis_size("ctx")
    ctx_index = lax.axis_index("ctx")
    lag_steps = jnp.arange(row_count, dtype=jnp.float32)
    weight = residues * jnp.sqrt(1.0 - jnp.exp(-2.0 * rates))
    full_powers = jnp.exp(-rates[:, :, None] * lag_steps)
    tail_powers = full_powers[:, :, ::-1] * jnp.exp(-rates)[:, :, None]
    no_prior = jnp.zeros((2,) + feats_wide.shape[1:], jnp.float32)
    blind = short_conv(jnp.concatenate([no_prior, feats_wide], axis=0), short_filter)
    blind_product = (blind[:, 1] * blind[:, 2]).astype(jnp.bfloat16).T.astype(jnp.float32)
    late_state = jnp.einsum(
        "ct,cmt->cm", blind_product[:, 2:], tail_powers[:, :, 2:], precision=highest
    )
    mode_count = late_state.shape[1]
    head_rows = feats_wide[:2, 1:, :].reshape(4, chan_count)
    tail_rows = feats_wide[-2:].reshape(6, chan_count)
    payload = jnp.concatenate([late_state.T, head_rows, tail_rows], axis=0)
    received = gather_by_exchange(payload, "ctx", concat_axis=0)
    conv_blind = modal_conv(blind_product, weight, rates, full_powers, 16)
    long_taps = jnp.sum(weight[:, :, None] * full_powers, axis=1)
    later_taps = jnp.concatenate([jnp.zeros_like(long_taps[:, :1]), long_taps[:, :-1]], axis=1)
    received, conv_blind, long_taps, later_taps, full_powers = lax.optimization_barrier(
        (received, conv_blind, long_taps, later_taps, full_powers)
    )
    late_all = received[:, :mode_count]
    head_all = received[:, mode_count : mode_count + 4].reshape(ctx_count, 2, 2, chan_count)
    tail_all = received[:, mode_count + 4 :].reshape(ctx_count, 2, 3, chan_count)
    prev_tail = jnp.concatenate([jnp.zeros_like(tail_all[:1]), tail_all[:-1]], axis=0)
    edge_joined = jnp.concatenate([prev_tail[:, :, 1:], head_all], axis=1)
    taps = short_filter[:, 1:, :]
    edge_short = taps[0] * edge_joined[:, 2:] + taps[1] * edge_joined[:, 1:3] + taps[2] * edge_joined[:, :2]
    edge_product = (edge_short[:, :, 0] * edge_short[:, :, 1]).astype(jnp.bfloat16).astype(jnp.float32)
    first_powers = tail_powers[:, :, 0].T
    second_powers = tail_powers[:, :, 1].T
    gathered_states = (
        late_all
        + edge_product[:, 0:1, :] * first_powers[None]
        + edge_product[:, 1:2, :] * second_powers[None]
    )
    shard_steps = jnp.arange(ctx_count, dtype=jnp.float32)
    gap_count = ctx_index.astype(jnp.float32) - 1.0 - shard_steps
    decay = jnp.where(
        (gap_count >= 0.0)[:, None, None],
        jnp.exp(-rates.T[None] * row_count * jnp.maximum(gap_count, 0.0)[:, None, None]),
        0.0,
    )
    start_state = jnp.sum(decay * gathered_states, axis=0).T
    own_prior = lax.dynamic_index_in_dim(prev_tail, ctx_index, 0, keepdims=False)
    own_edge = short_conv(jnp.concatenate([own_prior, feats_wide[:2]], axis=0), short_filter)
    own_edge_product = (own_edge[:, 1] * own_edge[:, 2]).astype(jnp.bfloat16).astype(jnp.float32)
    delta = own_edge_product - blind_product[:, :2].T
    start_part = jnp.sum((weight * start_state)[:, :, None] * full_powers, axis=1)
    conv_out = (
        conv_blind + start_part + long_taps * delta[0][:, None] + later_taps * delta[1][:, None]
    ).T
    short_query = jnp.concatenate([own_edge[:, 0], blind[2:, 0]], axis=0)
    gated = (short_query * conv_out).astype(jnp.bfloat16)
    tp_count = lax.axis_size("tp")
    pair_weight = out_weight.reshape(chan_count, tp_count // 2, 2, width_all // tp_count)
    even_part = jnp.einsum(
        "tc,cid->itd", gated, pair_weight[:, :, 0], preferred_element_type=jnp.float32
    )
    odd_part = jnp.einsum(
        "tc,cid->itd", gated, pair_weight[:, :, 1], preferred_element_type=jnp.float32
    )
    is_even = lax.axis_index("tp") % 2 == 0
    kept = jnp.where(is_even, even_part, odd_part)
    given = jnp.where(is_even, odd_part, even_part).astype(jnp.bfloat16)
    from_sibling = lax.ppermute(given, "tp", [(i, i ^ 1) for i in range(tp_count)])
    chip_sum = (kept + from_sibling.astype(jnp.float32)).astype(jnp.bfloat16)
    same_core = [[2 * i + c for i in range(tp_count // 2)] for c in range(2)]
    received = lax.all_to_all(
        chip_sum, "tp", split_axis=0, concat_axis=0, axis_index_groups=same_core
    )
    own_share = jnp.sum(received.astype(jnp.float32), axis=0)
    hyena_out = (resid_in.astype(jnp.float32) + own_share).astype(jnp.bfloat16)
    full_rows = gather_by_exchange(hyena_out, "tp").reshape(row_count, width_all)
    wide = full_rows.astype(jnp.float32)
    mean_square = jnp.mean(wide * wide, axis=1, keepdims=True)
    scaled = (wide * norm_gain).astype(jnp.bfloat16)
    projected = (
        jnp.dot(
            scaled, attn_weight.reshape(width_all, 3 * chan_count), preferred_element_type=jnp.float32
        )
        * lax.rsqrt(mean_square + eps_norm)
    ).reshape(row_count, 3, chan_count)
    head_count = chan_count // HEAD_DIM
    first_pos = ctx_index * row_count
    positions = first_pos + jnp.arange(row_count, dtype=jnp.int32)
    queries = rotary_turn(
        projected[:, 0].reshape(row_count, head_count, HEAD_DIM), positions
    ).astype(jnp.bfloat16)
    keys_all = rotary_turn(
        projected[:, 1].reshape(row_count, head_count, HEAD_DIM), positions
    ).astype(jnp.bfloat16)
    values = projected[:, 2].astype(jnp.bfloat16)
    joined_kv = jnp.concatenate([keys_all.reshape(row_count, chan_count), values], axis=1)
    gathered_kv = gather_by_exchange(joined_kv, "ctx", concat_axis=0)
    gathered_kv = gathered_kv.reshape(ctx_count * row_count, 2 * chan_count)
    key_total = gathered_kv.shape[0]
    key_rows = gathered_kv[:, :chan_count].reshape(key_total, head_count, HEAD_DIM)
    value_rows = gathered_kv[:, chan_count:].reshape(key_total, head_count, HEAD_DIM)
    key_pos = jnp.arange(key_total, dtype=jnp.int32)
    scores = jnp.einsum(
        "shd,khd->hsk", queries, key_rows, preferred_element_type=jnp.float32
    ) * (1.0 / math.sqrt(HEAD_DIM))
    allowed = (positions[:, None] >= key_pos[None, :])[None]
    masked = jnp.where(allowed, scores, mask_fill)
    run_peak = jnp.max(masked, axis=2, keepdims=True)
    probs = jnp.where(allowed, jnp.exp(masked - run_peak), 0.0)
    denom = jnp.sum(probs, axis=2, keepdims=True)
    summed = jnp.einsum(
        "hsk,khd->hsd", probs.astype(jnp.bfloat16), value_rows, preferred_element_type=jnp.float32
    )
    heads_out = summed / denom
    context = heads_out.transpose(1, 0, 2).reshape(row_count, chan_count).astype(jnp.bfloat16)
    return (hyena_out, context)


def solution(mesh):
    in_specs = (
        P("ctx", "tp"),
        P("ctx", None, "tp"),
        P(None, None, "tp"),
        P("tp", None),
        P("tp", None),
        P("tp", None),
        P(),
        P(None, None, "tp"),
    )
    out_specs = (P("ctx", "tp"), P("ctx", "tp"))
    return jax.shard_map(
        per_device, mesh=mesh, in_specs=in_specs, out_specs=out_specs, check_vma=False
    )
```

```python
import math

import jax
import jax.numpy as jnp
from jax import lax
from jax.sharding import PartitionSpec as P

HEAD_DIM = 128


eps_norm = 1e-05
rope_base = 10000.0
mask_fill = -1e30
highest = lax.Precision.HIGHEST


def gather_by_exchange(block, axis, concat_axis=1):
    count = lax.axis_size(axis)
    copies = jnp.broadcast_to(block[None], (count,) + block.shape)
    return lax.all_to_all(copies, axis, split_axis=0, concat_axis=concat_axis, tiled=False)


def toeplitz_lower(filter_taps):
    chan_count, block_size = filter_taps.shape
    padded = jnp.concatenate(
        [jnp.zeros((chan_count, block_size - 1), jnp.float32), filter_taps], axis=1
    )
    flipped = padded[:, ::-1]
    tiled = jnp.tile(flipped, (1, block_size))
    offset = block_size - 1
    window = tiled[:, offset : offset + block_size * (2 * block_size - 2)]
    return window.reshape(chan_count, block_size, 2 * block_size - 2)[:, :, :block_size]


def modal_conv(signal, residues, rates, start_state, block_limit=128):
    chan_count, length = signal.shape
    block_size = math.gcd(length, block_limit)
    block_count = length // block_size
    weight = residues * jnp.sqrt(1.0 - jnp.exp(-2.0 * rates))
    lag_steps = jnp.arange(block_size, dtype=jnp.float32)
    powers = jnp.exp(-rates[:, :, None] * lag_steps)
    filter_taps = jnp.sum(weight[:, :, None] * powers, axis=1)
    toeplitz = toeplitz_lower(filter_taps)
    blocks = signal.reshape(chan_count, block_count, block_size)
    inner_part = jnp.sum(toeplitz[:, None, :, :] * blocks[:, :, None, :], axis=3)
    tail_powers = jnp.exp(-rates[:, :, None] * (block_size - lag_steps))
    end_states = jnp.sum(blocks[:, :, None, :] * tail_powers[:, None, :, :], axis=3)
    block_steps = jnp.arange(block_count, dtype=jnp.float32)
    gap_count = block_steps[:, None] - 1.0 - block_steps[None, :]
    live_mask = gap_count >= 0.0
    carry_mat = jnp.where(
        live_mask, jnp.exp(-rates[:, :, None, None] * block_size * jnp.maximum(gap_count, 0.0)), 0.0
    )
    states = jnp.sum(carry_mat * end_states.transpose(0, 2, 1)[:, :, None, :], axis=3).transpose(0, 2, 1)
    states = (
        states
        + jnp.exp(-rates[:, None, :] * block_size * block_steps[None, :, None])
        * start_state[:, None, :]
    )
    cross_part = jnp.sum((states * weight[:, None, :])[:, :, :, None] * powers[:, None, :, :], axis=2)
    return (inner_part + cross_part).reshape(chan_count, length)


def short_conv(joined, short_filter):
    row_count = joined.shape[0] - 2
    return (
        short_filter[0] * joined[2:]
        + short_filter[1] * joined[1 : row_count + 1]
        + short_filter[2] * joined[:row_count]
    )


def rotary_turn(vectors, positions):
    half_dim = vectors.shape[-1] // 2
    frequency = rope_base ** (-jnp.arange(half_dim, dtype=jnp.float32) * 2.0 / vectors.shape[-1])
    angles = positions.astype(jnp.float32)[:, None] * frequency[None, :]
    cosine = jnp.cos(angles)[:, None, :]
    sine_part = jnp.sin(angles)[:, None, :]
    first_half = vectors[..., :half_dim]
    second = vectors[..., half_dim:]
    return jnp.concatenate(
        [first_half * cosine - second * sine_part, second * cosine + first_half * sine_part],
        axis=-1,
    )


def per_device(resid_in, feats, short_filter, residues, rates, out_weight, norm_gain, attn_weight):
    row_count, chan_count = resid_in.shape
    width_all = out_weight.shape[1]
    feats_wide = feats.astype(jnp.float32)
    ctx_count = lax.axis_size("ctx")
    ctx_index = lax.axis_index("ctx")
    lag_steps = jnp.arange(row_count, dtype=jnp.float32)
    tail_powers = jnp.exp(-rates[:, :, None] * (row_count - lag_steps))
    no_prior = jnp.zeros((2,) + feats_wide.shape[1:], jnp.float32)
    blind = short_conv(jnp.concatenate([no_prior, feats_wide], axis=0), short_filter)
    blind_product = (blind[:, 1] * blind[:, 2]).astype(jnp.bfloat16).T.astype(jnp.float32)
    late_state = jnp.einsum(
        "ct,cmt->cm", blind_product[:, 2:], tail_powers[:, :, 2:], precision=highest
    )
    mode_count = late_state.shape[1]
    head_rows = feats_wide[:2, 1:, :].reshape(4, chan_count)
    tail_rows = feats_wide[-2:].reshape(6, chan_count)
    payload = jnp.concatenate([late_state.T, head_rows, tail_rows], axis=0)
    received = gather_by_exchange(payload, "ctx", concat_axis=0)
    conv_blind = modal_conv(
        blind_product, residues, rates, jnp.zeros_like(rates), block_limit=16
    )
    weight = residues * jnp.sqrt(1.0 - jnp.exp(-2.0 * rates))
    full_powers = jnp.exp(-rates[:, :, None] * lag_steps)
    long_taps = jnp.sum(weight[:, :, None] * full_powers, axis=1)
    later_taps = jnp.concatenate([jnp.zeros_like(long_taps[:, :1]), long_taps[:, :-1]], axis=1)
    received, conv_blind, long_taps, later_taps, full_powers = lax.optimization_barrier(
        (received, conv_blind, long_taps, later_taps, full_powers)
    )
    late_all = received[:, :mode_count]
    head_all = received[:, mode_count : mode_count + 4].reshape(ctx_count, 2, 2, chan_count)
    tail_all = received[:, mode_count + 4 :].reshape(ctx_count, 2, 3, chan_count)
    prev_tail = jnp.concatenate([jnp.zeros_like(tail_all[:1]), tail_all[:-1]], axis=0)
    edge_joined = jnp.concatenate([prev_tail[:, :, 1:], head_all], axis=1)
    taps = short_filter[:, 1:, :]
    edge_short = taps[0] * edge_joined[:, 2:] + taps[1] * edge_joined[:, 1:3] + taps[2] * edge_joined[:, :2]
    edge_product = (edge_short[:, :, 0] * edge_short[:, :, 1]).astype(jnp.bfloat16).astype(jnp.float32)
    first_powers = tail_powers[:, :, 0].T
    second_powers = tail_powers[:, :, 1].T
    gathered_states = (
        late_all
        + edge_product[:, 0:1, :] * first_powers[None]
        + edge_product[:, 1:2, :] * second_powers[None]
    )
    shard_steps = jnp.arange(ctx_count, dtype=jnp.float32)
    gap_count = ctx_index.astype(jnp.float32) - 1.0 - shard_steps
    decay = jnp.where(
        (gap_count >= 0.0)[:, None, None],
        jnp.exp(-rates.T[None] * row_count * jnp.maximum(gap_count, 0.0)[:, None, None]),
        0.0,
    )
    start_state = jnp.sum(decay * gathered_states, axis=0).T
    own_prior = lax.dynamic_index_in_dim(prev_tail, ctx_index, 0, keepdims=False)
    own_edge = short_conv(jnp.concatenate([own_prior, feats_wide[:2]], axis=0), short_filter)
    own_edge_product = (own_edge[:, 1] * own_edge[:, 2]).astype(jnp.bfloat16).astype(jnp.float32)
    delta = own_edge_product - blind_product[:, :2].T
    start_part = jnp.sum((weight * start_state)[:, :, None] * full_powers, axis=1)
    conv_out = (
        conv_blind + start_part + long_taps * delta[0][:, None] + later_taps * delta[1][:, None]
    ).T
    short_query = jnp.concatenate([own_edge[:, 0], blind[2:, 0]], axis=0)
    gated = (short_query * conv_out).astype(jnp.bfloat16)
    tp_count = lax.axis_size("tp")
    pair_weight = out_weight.reshape(chan_count, tp_count // 2, 2, width_all // tp_count)
    even_part = jnp.einsum(
        "tc,cid->itd", gated, pair_weight[:, :, 0], preferred_element_type=jnp.float32
    )
    odd_part = jnp.einsum(
        "tc,cid->itd", gated, pair_weight[:, :, 1], preferred_element_type=jnp.float32
    )
    is_even = lax.axis_index("tp") % 2 == 0
    kept = jnp.where(is_even, even_part, odd_part)
    given = jnp.where(is_even, odd_part, even_part).astype(jnp.bfloat16)
    from_sibling = lax.ppermute(given, "tp", [(i, i ^ 1) for i in range(tp_count)])
    chip_sum = (kept + from_sibling.astype(jnp.float32)).astype(jnp.bfloat16)
    same_core = [[2 * i + c for i in range(tp_count // 2)] for c in range(2)]
    received = lax.all_to_all(
        chip_sum, "tp", split_axis=0, concat_axis=0, axis_index_groups=same_core
    )
    own_share = jnp.sum(received.astype(jnp.float32), axis=0)
    hyena_out = (resid_in.astype(jnp.float32) + own_share).astype(jnp.bfloat16)
    full_rows = gather_by_exchange(hyena_out, "tp").reshape(row_count, width_all)
    wide = full_rows.astype(jnp.float32)
    mean_square = jnp.mean(wide * wide, axis=1, keepdims=True)
    scaled = (wide * norm_gain).astype(jnp.bfloat16)
    projected = (
        jnp.dot(
            scaled, attn_weight.reshape(width_all, 3 * chan_count), preferred_element_type=jnp.float32
        )
        * lax.rsqrt(mean_square + eps_norm)
    ).reshape(row_count, 3, chan_count)
    head_count = chan_count // HEAD_DIM
    first_pos = ctx_index * row_count
    positions = first_pos + jnp.arange(row_count, dtype=jnp.int32)
    queries = rotary_turn(
        projected[:, 0].reshape(row_count, head_count, HEAD_DIM), positions
    ).astype(jnp.bfloat16)
    keys_all = rotary_turn(
        projected[:, 1].reshape(row_count, head_count, HEAD_DIM), positions
    ).astype(jnp.bfloat16)
    values = projected[:, 2].astype(jnp.bfloat16)
    joined_kv = jnp.concatenate([keys_all.reshape(row_count, chan_count), values], axis=1)
    gathered_kv = gather_by_exchange(joined_kv, "ctx", concat_axis=0)
    gathered_kv = gathered_kv.reshape(ctx_count * row_count, 2 * chan_count)
    key_total = gathered_kv.shape[0]
    key_rows = gathered_kv[:, :chan_count].reshape(key_total, head_count, HEAD_DIM)
    value_rows = gathered_kv[:, chan_count:].reshape(key_total, head_count, HEAD_DIM)
    key_pos = jnp.arange(key_total, dtype=jnp.int32)
    scores = jnp.einsum(
        "shd,khd->hsk", queries, key_rows, preferred_element_type=jnp.float32
    ) * (1.0 / math.sqrt(HEAD_DIM))
    allowed = (positions[:, None] >= key_pos[None, :])[None]
    masked = jnp.where(allowed, scores, mask_fill)
    run_peak = jnp.max(masked, axis=2, keepdims=True)
    probs = jnp.where(allowed, jnp.exp(masked - run_peak), 0.0)
    denom = jnp.sum(probs, axis=2, keepdims=True)
    summed = jnp.einsum(
        "hsk,khd->hsd", probs.astype(jnp.bfloat16), value_rows, preferred_element_type=jnp.float32
    )
    heads_out = summed / denom
    context = heads_out.transpose(1, 0, 2).reshape(row_count, chan_count).astype(jnp.bfloat16)
    return (hyena_out, context)


def solution(mesh):
    in_specs = (
        P("ctx", "tp"),
        P("ctx", None, "tp"),
        P(None, None, "tp"),
        P("tp", None),
        P("tp", None),
        P("tp", None),
        P(),
        P(None, None, "tp"),
    )
    out_specs = (P("ctx", "tp"), P("ctx", "tp"))
    return jax.shard_map(
        per_device, mesh=mesh, in_specs=in_specs, out_specs=out_specs, check_vma=False
    )
```

```python
import math

import jax
import jax.numpy as jnp
from jax import lax
from jax.sharding import PartitionSpec as P

HEAD_DIM = 128


eps_norm = 1e-05
rope_base = 10000.0
mask_fill = -1e30
highest = lax.Precision.HIGHEST


def gather_by_exchange(block, axis, concat_axis=1):
    count = lax.axis_size(axis)
    copies = jnp.broadcast_to(block[None], (count,) + block.shape)
    return lax.all_to_all(copies, axis, split_axis=0, concat_axis=concat_axis, tiled=False)


def toeplitz_lower(filter_taps):
    chan_count, block_size = filter_taps.shape
    padded = jnp.concatenate(
        [jnp.zeros((chan_count, block_size - 1), jnp.float32), filter_taps], axis=1
    )
    flipped = padded[:, ::-1]
    tiled = jnp.tile(flipped, (1, block_size))
    offset = block_size - 1
    window = tiled[:, offset : offset + block_size * (2 * block_size - 2)]
    return window.reshape(chan_count, block_size, 2 * block_size - 2)[:, :, :block_size]


def modal_conv(signal, residues, rates, start_state, block_limit=128):
    chan_count, length = signal.shape
    block_size = math.gcd(length, block_limit)
    block_count = length // block_size
    weight = residues * jnp.sqrt(1.0 - jnp.exp(-2.0 * rates))
    lag_steps = jnp.arange(block_size, dtype=jnp.float32)
    powers = jnp.exp(-rates[:, :, None] * lag_steps)
    filter_taps = jnp.sum(weight[:, :, None] * powers, axis=1)
    toeplitz = toeplitz_lower(filter_taps)
    blocks = signal.reshape(chan_count, block_count, block_size)
    inner_part = jnp.einsum("cij,cnj->cni", toeplitz, blocks, precision=highest)
    tail_powers = jnp.exp(-rates[:, :, None] * (block_size - lag_steps))
    end_states = jnp.einsum("cnj,cmj->cnm", blocks, tail_powers, precision=highest)
    block_steps = jnp.arange(block_count, dtype=jnp.float32)
    gap_count = block_steps[:, None] - 1.0 - block_steps[None, :]
    live_mask = gap_count >= 0.0
    carry_mat = jnp.where(
        live_mask, jnp.exp(-rates[:, :, None, None] * block_size * jnp.maximum(gap_count, 0.0)), 0.0
    )
    states = jnp.einsum("cmnk,ckm->cnm", carry_mat, end_states, precision=highest)
    cross_part = jnp.einsum("cnm,cmi->cni", states * weight[:, None, :], powers, precision=highest)
    return (inner_part + cross_part).reshape(chan_count, length)


def short_conv(joined, short_filter):
    row_count = joined.shape[0] - 2
    return (
        short_filter[0] * joined[2:]
        + short_filter[1] * joined[1 : row_count + 1]
        + short_filter[2] * joined[:row_count]
    )


def rotary_turn(vectors, positions):
    half_dim = vectors.shape[-1] // 2
    frequency = rope_base ** (-jnp.arange(half_dim, dtype=jnp.float32) * 2.0 / vectors.shape[-1])
    angles = positions.astype(jnp.float32)[:, None] * frequency[None, :]
    cosine = jnp.cos(angles)[:, None, :]
    sine_part = jnp.sin(angles)[:, None, :]
    first_half = vectors[..., :half_dim]
    second = vectors[..., half_dim:]
    return jnp.concatenate(
        [first_half * cosine - second * sine_part, second * cosine + first_half * sine_part],
        axis=-1,
    )


def per_device(resid_in, feats, short_filter, residues, rates, out_weight, norm_gain, attn_weight):
    row_count, chan_count = resid_in.shape
    width_all = out_weight.shape[1]
    feats_wide = feats.astype(jnp.float32)
    ctx_count = lax.axis_size("ctx")
    ctx_index = lax.axis_index("ctx")
    lag_steps = jnp.arange(row_count, dtype=jnp.float32)
    tail_powers = jnp.exp(-rates[:, :, None] * (row_count - lag_steps))
    no_prior = jnp.zeros((2,) + feats_wide.shape[1:], jnp.float32)
    blind = short_conv(jnp.concatenate([no_prior, feats_wide], axis=0), short_filter)
    blind_product = (blind[:, 1] * blind[:, 2]).astype(jnp.bfloat16).T.astype(jnp.float32)
    late_state = jnp.einsum(
        "ct,cmt->cm", blind_product[:, 2:], tail_powers[:, :, 2:], precision=highest
    )
    mode_count = late_state.shape[1]
    head_rows = feats_wide[:2, 1:, :].reshape(4, chan_count)
    tail_rows = feats_wide[-2:].reshape(6, chan_count)
    payload = jnp.concatenate([late_state.T, head_rows, tail_rows], axis=0)
    received = gather_by_exchange(payload, "ctx", concat_axis=0)
    conv_blind = modal_conv(
        blind_product, residues, rates, jnp.zeros_like(rates), block_limit=16
    )
    weight = residues * jnp.sqrt(1.0 - jnp.exp(-2.0 * rates))
    full_powers = jnp.exp(-rates[:, :, None] * lag_steps)
    long_taps = jnp.sum(weight[:, :, None] * full_powers, axis=1)
    later_taps = jnp.concatenate([jnp.zeros_like(long_taps[:, :1]), long_taps[:, :-1]], axis=1)
    received, conv_blind, long_taps, later_taps, full_powers = lax.optimization_barrier(
        (received, conv_blind, long_taps, later_taps, full_powers)
    )
    late_all = received[:, :mode_count]
    head_all = received[:, mode_count : mode_count + 4].reshape(ctx_count, 2, 2, chan_count)
    tail_all = received[:, mode_count + 4 :].reshape(ctx_count, 2, 3, chan_count)
    prev_tail = jnp.concatenate([jnp.zeros_like(tail_all[:1]), tail_all[:-1]], axis=0)
    edge_joined = jnp.concatenate([prev_tail[:, :, 1:], head_all], axis=1)
    taps = short_filter[:, 1:, :]
    edge_short = taps[0] * edge_joined[:, 2:] + taps[1] * edge_joined[:, 1:3] + taps[2] * edge_joined[:, :2]
    edge_product = (edge_short[:, :, 0] * edge_short[:, :, 1]).astype(jnp.bfloat16).astype(jnp.float32)
    first_powers = tail_powers[:, :, 0].T
    second_powers = tail_powers[:, :, 1].T
    gathered_states = (
        late_all
        + edge_product[:, 0:1, :] * first_powers[None]
        + edge_product[:, 1:2, :] * second_powers[None]
    )
    shard_steps = jnp.arange(ctx_count, dtype=jnp.float32)
    gap_count = ctx_index.astype(jnp.float32) - 1.0 - shard_steps
    decay = jnp.where(
        (gap_count >= 0.0)[:, None, None],
        jnp.exp(-rates.T[None] * row_count * jnp.maximum(gap_count, 0.0)[:, None, None]),
        0.0,
    )
    start_state = jnp.sum(decay * gathered_states, axis=0).T
    own_prior = lax.dynamic_index_in_dim(prev_tail, ctx_index, 0, keepdims=False)
    own_edge = short_conv(jnp.concatenate([own_prior, feats_wide[:2]], axis=0), short_filter)
    own_edge_product = (own_edge[:, 1] * own_edge[:, 2]).astype(jnp.bfloat16).astype(jnp.float32)
    delta = own_edge_product - blind_product[:, :2].T
    start_part = jnp.sum((weight * start_state)[:, :, None] * full_powers, axis=1)
    conv_out = (
        conv_blind + start_part + long_taps * delta[0][:, None] + later_taps * delta[1][:, None]
    ).T
    short_query = jnp.concatenate([own_edge[:, 0], blind[2:, 0]], axis=0)
    gated = (short_query * conv_out).astype(jnp.bfloat16)
    tp_count = lax.axis_size("tp")
    pair_weight = out_weight.reshape(chan_count, tp_count // 2, 2, width_all // tp_count)
    even_part = jnp.einsum(
        "tc,cid->itd", gated, pair_weight[:, :, 0], preferred_element_type=jnp.float32
    )
    odd_part = jnp.einsum(
        "tc,cid->itd", gated, pair_weight[:, :, 1], preferred_element_type=jnp.float32
    )
    is_even = lax.axis_index("tp") % 2 == 0
    kept = jnp.where(is_even, even_part, odd_part)
    given = jnp.where(is_even, odd_part, even_part).astype(jnp.bfloat16)
    from_sibling = lax.ppermute(given, "tp", [(i, i ^ 1) for i in range(tp_count)])
    chip_sum = (kept + from_sibling.astype(jnp.float32)).astype(jnp.bfloat16)
    same_core = [[2 * i + c for i in range(tp_count // 2)] for c in range(2)]
    received = lax.all_to_all(
        chip_sum, "tp", split_axis=0, concat_axis=0, axis_index_groups=same_core
    )
    own_share = jnp.sum(received.astype(jnp.float32), axis=0)
    hyena_out = (resid_in.astype(jnp.float32) + own_share).astype(jnp.bfloat16)
    full_rows = gather_by_exchange(hyena_out, "tp").reshape(row_count, width_all)
    wide = full_rows.astype(jnp.float32)
    mean_square = jnp.mean(wide * wide, axis=1, keepdims=True)
    scaled = (wide * norm_gain).astype(jnp.bfloat16)
    projected = (
        jnp.dot(
            scaled, attn_weight.reshape(width_all, 3 * chan_count), preferred_element_type=jnp.float32
        )
        * lax.rsqrt(mean_square + eps_norm)
    ).reshape(row_count, 3, chan_count)
    head_count = chan_count // HEAD_DIM
    first_pos = ctx_index * row_count
    positions = first_pos + jnp.arange(row_count, dtype=jnp.int32)
    queries = rotary_turn(
        projected[:, 0].reshape(row_count, head_count, HEAD_DIM), positions
    ).astype(jnp.bfloat16)
    keys_all = rotary_turn(
        projected[:, 1].reshape(row_count, head_count, HEAD_DIM), positions
    ).astype(jnp.bfloat16)
    values = projected[:, 2].astype(jnp.bfloat16)
    joined_kv = jnp.concatenate([keys_all.reshape(row_count, chan_count), values], axis=1)
    gathered_kv = gather_by_exchange(joined_kv, "ctx", concat_axis=0)
    gathered_kv = gathered_kv.reshape(ctx_count * row_count, 2 * chan_count)
    key_total = gathered_kv.shape[0]
    key_rows = gathered_kv[:, :chan_count].reshape(key_total, head_count, HEAD_DIM)
    value_rows = gathered_kv[:, chan_count:].reshape(key_total, head_count, HEAD_DIM)
    key_pos = jnp.arange(key_total, dtype=jnp.int32)
    scores = jnp.einsum(
        "shd,khd->hsk", queries, key_rows, preferred_element_type=jnp.float32
    ) * (1.0 / math.sqrt(HEAD_DIM))
    allowed = (positions[:, None] >= key_pos[None, :])[None]
    masked = jnp.where(allowed, scores, mask_fill)
    run_peak = jnp.max(masked, axis=2, keepdims=True)
    probs = jnp.where(allowed, jnp.exp(masked - run_peak), 0.0)
    denom = jnp.sum(probs, axis=2, keepdims=True)
    summed = jnp.einsum(
        "hsk,khd->hsd", probs.astype(jnp.bfloat16), value_rows, preferred_element_type=jnp.float32
    )
    heads_out = summed / denom
    context = heads_out.transpose(1, 0, 2).reshape(row_count, chan_count).astype(jnp.bfloat16)
    return (hyena_out, context)


def solution(mesh):
    in_specs = (
        P("ctx", "tp"),
        P("ctx", None, "tp"),
        P(None, None, "tp"),
        P("tp", None),
        P("tp", None),
        P("tp", None),
        P(),
        P(None, None, "tp"),
    )
    out_specs = (P("ctx", "tp"), P("ctx", "tp"))
    return jax.shard_map(
        per_device, mesh=mesh, in_specs=in_specs, out_specs=out_specs, check_vma=False
    )
```
